256 devices in a mesh: req: 32 (over z, y_hi, core), tp: 8 (over x, y_lo).
Axes of the slice: x: 4, y: 4 (y_hi: 2, y_lo: 2; y = y_hi * 2 + y_lo), z: 8, core: 2. Of those that a mesh axis runs over, the one named last changes fastest.
Arguments:
- tokens: bfloat16 [16384, 1024], P(('req', 'tp')), may hold values from -6 to 6
- w_qkv: bfloat16 [1024, 3, 1024], P(None, None, 'tp'), may hold values from -0.1875 to 0.1875
- w_out: bfloat16 [1024, 1024], P('tp'), may hold values from -0.75 to 0.75
- w_up: bfloat16 [1024, 4096], P(None, 'tp'), may hold values from -0.1875 to 0.1875
- b_up: float32 [4096], P('tp'), may hold values from -4 to 4
- w_down: bfloat16 [4096, 1024], P('tp'), may hold values from -0.09375 to 0.09375
- b_down: float32 [1024], replicated, may hold values from -3 to 3
- ln1_gain: float32 [1024], replicated, may hold values from 0.5 to 1.5
- ln1_bias: float32 [1024], replicated, may hold values from -3 to 3
- ln2_gain: float32 [1024], replicated, may hold values from 0.5 to 1.5
- ln2_bias: float32 [1024], replicated, may hold values from -3 to 3
- kv_cache: bfloat16 [2, 32, 16384, 1024], P(None, None, 'req', 'tp'), may hold values from -122 to 122
- cache_len: int32 [32], replicated, may hold values from 0 to 16384, as said below
- span_len: int32 [32], replicated, may hold values from 1 to 512, as said below
Outputs:
- output: bfloat16 [16384, 1024], P(('req', 'tp'))
The draws below stay inside these ranges and needn't reach their ends.
Inputs may be any that keep to these rules, and one draw needn't show every extreme that they name: The first cache_len[r] positions of request r hold its keys and values; some request has 16384. Slots from span_len[r] on are padding whose keys are not attended to; some request has 512.
All inputs are finite; a program needn't handle non-finite values.
Results may differ from the reference program's by a relative error of at most 0.015.
Values may be sent and summed in bfloat16 or wider, within the bound.
No kernel may reach another device: no remote copies, remote signals or barrier semaphores. Data moves between devices by JAX's collectives and lax.ppermute only.
A program may use at most 128 MiB of HBM per device.

```python
import jax
import jax.numpy as jnp
from jax import lax

D = 1024
HEADS = 16
HEAD_DIM = 64
FF = 4096
SPAN = 512
CAP = 16384
REQUESTS = 32
TOKENS = 16384
BLOCK = 512
N_REQ = 32


def draw_kv_cache(key, part):
    full_shape = (2, REQUESTS, CAP, D)
    first = jax.random.fold_in(jax.random.fold_in(key, 11), 0)
    result = 2.0 * jax.random.normal(first, full_shape, jnp.float32)
    return result.astype(jnp.bfloat16)


def draw_cache_len(key, part):
    first, second, third = jax.random.split(jax.random.fold_in(key, 23), 3)
    background = jax.random.randint(first, (REQUESTS,), 0, CAP + 1)
    shifts = jax.random.randint(second, (REQUESTS,), 0, 3)
    lengths = background // jnp.left_shift(jnp.ones_like(shifts), shifts)
    longest = jax.random.randint(third, (), 0, REQUESTS)
    return jnp.where(jnp.arange(REQUESTS) == longest, CAP, lengths).astype(jnp.int32)


def draw_span_len(key, part):
    first, second = jax.random.split(jax.random.fold_in(key, 37), 2)
    lengths = jax.random.randint(first, (REQUESTS,), 1, SPAN + 1)
    longest = jax.random.randint(second, (), 0, REQUESTS)
    return jnp.where(jnp.arange(REQUESTS) == longest, SPAN, lengths).astype(jnp.int32)


def block_scale(stream_key, shape, cuts, smallest, largest):
    level, own = 1.0, jax.random.fold_in(stream_key, 6)
    for position, blocks in cuts:
        draws = jnp.exp(jax.random.uniform(jax.random.fold_in(own, position), (blocks,), jnp.float32, smallest / len(cuts), largest / len(cuts)))
        level = level * jnp.repeat(draws, shape[position] // blocks).reshape([-1 if axis == position else 1 for axis in range(len(shape))])
    return level


def noise(rng, shape, scale, reach, pieces=(), kind=jnp.bfloat16):
    values = scale * jax.random.normal(rng, shape, jnp.float32)
    if pieces:
        values = values * block_scale(rng, shape, pieces, -0.22, 0.18)
    return jnp.clip(values, -reach, reach).astype(kind)


def setup_inputs(seed: int = 0) -> dict:
    streams_of = jax.random.split(jax.random.key(seed), 15)
    tokens = noise(streams_of[0], (TOKENS, D), 1.0, 6.0, ((0, 256),))
    w_qkv = noise(streams_of[1], (D, 3, D), D ** -0.5, 0.1875, ((2, 8),))
    w_out = noise(streams_of[2], (D, D), HEAD_DIM ** -0.5, 0.75, ((0, 8),))
    w_up = noise(streams_of[3], (D, FF), D ** -0.5, 0.1875, ((1, 8),))
    b_up = noise(streams_of[4], (FF,), 1.0, 4.0, ((0, 8),), jnp.float32)
    w_down = noise(streams_of[5], (FF, D), FF ** -0.5, 0.09375, ((0, 8),))
    b_down = noise(streams_of[6], (D,), 0.5, 3.0, (), jnp.float32)
    ln1_gain = jnp.clip(1.0 + 0.1 * jax.random.normal(streams_of[7], (D,), jnp.float32), 0.5, 1.5)
    ln1_bias = noise(streams_of[8], (D,), 0.5, 3.0, (), jnp.float32)
    ln2_gain = jnp.clip(1.0 + 0.1 * jax.random.normal(streams_of[9], (D,), jnp.float32), 0.5, 1.5)
    ln2_bias = noise(streams_of[10], (D,), 0.5, 3.0, (), jnp.float32)
    kv_cache = draw_kv_cache(jax.random.fold_in(streams_of[14], 71), 0)
    cache_len = draw_cache_len(jax.random.fold_in(streams_of[14], 71), 0)
    span_len = draw_span_len(jax.random.fold_in(streams_of[14], 71), 0)
    return dict(tokens=tokens, w_qkv=w_qkv, w_out=w_out, w_up=w_up, b_up=b_up, w_down=w_down, b_down=b_down, ln1_gain=ln1_gain, ln1_bias=ln1_bias, ln2_gain=ln2_gain, ln2_bias=ln2_bias, kv_cache=kv_cache, cache_len=cache_len, span_len=span_len)


masked_score = -1e+30

def layer_norm(values, gain, bias):
    centre = lax.optimization_barrier(jnp.mean(values, axis=-1, keepdims=True))
    centred = values - centre
    variance = lax.optimization_barrier(jnp.mean(centred * centred, axis=-1, keepdims=True))
    return centred * lax.rsqrt(variance + 1e-05) * gain + bias

def partial_attention(queries, key_rows, value_rows, allowed):
    scores = jnp.einsum('chd,nhd->hcn', queries.astype(jnp.float32), key_rows.astype(jnp.float32)) * queries.shape[-1] ** (-0.5)
    scores = jnp.where(allowed[None], scores, masked_score)
    peaks = lax.optimization_barrier(jnp.max(scores, axis=-1))
    weights = jnp.where(allowed[None], jnp.exp(scores - peaks[..., None]), 0.0).astype(jnp.bfloat16)
    weight_sums = lax.optimization_barrier(jnp.sum(weights.astype(jnp.float32), axis=-1))
    blended = jnp.einsum('hcn,nhd->chd', weights.astype(jnp.float32), value_rows.astype(jnp.float32))
    return (peaks.T, weight_sums.T, blended.reshape(blended.shape[0], -1))

def merge_axis(peaks, weight_sums, blended, axis):
    highest = lax.optimization_barrier(jnp.max(peaks, axis=axis, keepdims=True))
    factors = jnp.exp(peaks - highest)
    sums_out = lax.optimization_barrier(jnp.sum(factors * weight_sums, axis=axis))
    spread = jnp.repeat(factors, blended.shape[-1] // peaks.shape[-1], axis=-1)
    blend_out = lax.optimization_barrier(jnp.sum(spread * blended, axis=axis))
    return (jnp.squeeze(highest, axis=axis), sums_out, blend_out)

def reference(tokens, w_qkv, w_out, w_up, b_up, w_down, b_down, ln1_gain, ln1_bias, ln2_gain, ln2_bias, kv_cache, cache_len, span_len):
    heads_qkv = jnp.dot(tokens, w_qkv.reshape(D, 3 * D), preferred_element_type=jnp.float32).astype(jnp.bfloat16)
    four_shape = (REQUESTS, SPAN, HEADS, HEAD_DIM)
    queries = heads_qkv[:, :D].reshape(four_shape)
    fresh_keys = heads_qkv[:, D:2 * D].reshape(four_shape)
    fresh_values = heads_qkv[:, 2 * D:].reshape(four_shape)
    cached = kv_cache.reshape(2, REQUESTS, N_REQ, BLOCK, HEADS, HEAD_DIM)
    positions = jnp.arange(SPAN, dtype=jnp.int32)
    block_starts = jnp.arange(N_REQ, dtype=jnp.int32) * BLOCK

    def per_request(items):
        own_queries, own_keys, own_values, cache_keys, cache_values, cached_count, fresh_count = items
        allowed = (positions[None, :] <= positions[:, None]) & (positions[None, :] < fresh_count)
        fresh = partial_attention(own_queries, own_keys, own_values, allowed)

        def per_block(block):
            block_keys, block_values, start_pos = block
            places = start_pos + jnp.arange(BLOCK, dtype=jnp.int32)
            block_allowed = jnp.broadcast_to((places < cached_count)[None, :], (SPAN, BLOCK))
            return partial_attention(own_queries, block_keys, block_values, block_allowed)
        blocks = lax.map(per_block, (cache_keys, cache_values, block_starts))
        joined = [jnp.concatenate([fresh[index][None], blocks[index]], axis=0) for index in range(3)]
        peaks, weight_sums, blended = merge_axis(joined[0], joined[1], joined[2], 0)
        return (blended / jnp.repeat(weight_sums, HEAD_DIM, axis=-1)).astype(jnp.bfloat16)
    attention = lax.map(per_request, (queries, fresh_keys, fresh_values, cached[0], cached[1], cache_len, span_len))
    attention = attention.reshape(TOKENS, D)
    projected = jnp.dot(attention, w_out, preferred_element_type=jnp.float32)
    normed = layer_norm(tokens.astype(jnp.float32) + projected, ln1_gain, ln1_bias).astype(jnp.bfloat16)
    hidden = jax.nn.gelu(jnp.dot(normed, w_up, preferred_element_type=jnp.float32) + b_up, approximate=False).astype(jnp.bfloat16)
    summed = jnp.dot(hidden, w_down, preferred_element_type=jnp.float32) + b_down + normed.astype(jnp.float32)
    return layer_norm(summed, ln2_gain, ln2_bias).astype(jnp.bfloat16)
```

```python
import jax
import jax.numpy as jnp
from jax import lax
from jax.sharding import PartitionSpec as P

HEAD_DIM = 64
BLOCK_GROUP = 4

masked_score = -1e30


def layer_norm(values, gain, bias):
    centre = jnp.mean(values, axis=-1, keepdims=True)
    centred = values - centre
    variance = jnp.mean(centred * centred, axis=-1, keepdims=True)
    return centred * lax.rsqrt(variance + 1e-05) * gain + bias


def partial_attention(queries, key_rows, value_rows, allowed):
    scores = jnp.einsum(
        "chd,nhd->hcn", queries, key_rows, preferred_element_type=jnp.float32
    ) * queries.shape[-1] ** (-0.5)
    scores = jnp.where(allowed[None], scores, masked_score)
    peaks = jnp.max(scores, axis=-1)
    weights = jnp.where(allowed[None], jnp.exp(scores - peaks[..., None]), 0.0).astype(jnp.bfloat16)
    weight_sums = jnp.sum(weights.astype(jnp.float32), axis=-1)
    blended = jnp.einsum("hcn,nhd->chd", weights, value_rows, preferred_element_type=jnp.float32)
    return (peaks.T, weight_sums.T, blended.reshape(blended.shape[0], -1))


def merge_axis(peaks, weight_sums, blended, axis):
    highest = jnp.max(peaks, axis=axis, keepdims=True)
    factors = jnp.exp(peaks - highest)
    sums_out = jnp.sum(factors * weight_sums, axis=axis)
    spread = jnp.repeat(factors, blended.shape[-1] // peaks.shape[-1], axis=-1)
    blend_out = jnp.sum(spread * blended, axis=axis)
    return (jnp.squeeze(highest, axis=axis), sums_out, blend_out)


def cache_partials(queries, keys, values, cached_count):
    total_blocks, block_width = keys.shape[0], keys.shape[1]
    group = BLOCK_GROUP if total_blocks % BLOCK_GROUP == 0 else 1

    def single(one_keys, one_values, block):
        places = block * block_width + jnp.arange(block_width, dtype=jnp.int32)
        allowed = jnp.broadcast_to((places < cached_count)[None, :], (queries.shape[0], block_width))
        return partial_attention(queries, one_keys, one_values, allowed)

    def grouped(items):
        return jax.vmap(single)(*items)

    def regroup(member):
        return member.reshape((total_blocks // group, group) + member.shape[1:])

    results = lax.map(
        grouped,
        (regroup(keys), regroup(values), regroup(jnp.arange(total_blocks, dtype=jnp.int32))),
    )
    return tuple(member.reshape((total_blocks,) + member.shape[2:]) for member in results)


def shards(
    tokens,
    w_qkv,
    w_out,
    w_up,
    b_up,
    w_down,
    b_down,
    ln1_gain,
    ln1_bias,
    ln2_gain,
    ln2_bias,
    kv_cache,
    cache_len,
    span_len,
):
    width_here = w_qkv.shape[2]
    heads_here = width_here // HEAD_DIM
    where_req = lax.axis_index("req")

    own_cache = lax.all_to_all(kv_cache, "req", split_axis=1, concat_axis=1, tiled=True)

    span_rows = lax.all_gather(tokens, "tp", axis=0, tiled=True)
    flat_qkv = w_qkv.reshape(w_qkv.shape[0], 3 * width_here)
    heads_qkv = jnp.dot(span_rows, flat_qkv, preferred_element_type=jnp.float32).astype(jnp.bfloat16)
    span = heads_qkv.shape[0]
    local_shape = (span, heads_here, HEAD_DIM)
    queries = heads_qkv[:, :width_here].reshape(local_shape)
    fresh_keys = heads_qkv[:, width_here : 2 * width_here].reshape(local_shape)
    fresh_values = heads_qkv[:, 2 * width_here :].reshape(local_shape)

    full_out = lax.all_gather(w_out, "tp", axis=0, tiled=True)
    full_up = lax.all_gather(w_up, "tp", axis=1, tiled=True)
    full_b_up = lax.all_gather(b_up, "tp", axis=0, tiled=True)
    full_down = lax.all_gather(w_down, "tp", axis=0, tiled=True)

    fresh_count = span_len[where_req]
    cached_count = cache_len[where_req]
    positions = jnp.arange(span, dtype=jnp.int32)
    allowed = (positions[None, :] <= positions[:, None]) & (positions[None, :] < fresh_count)
    fresh = partial_attention(queries, fresh_keys, fresh_values, allowed)

    total_blocks, block_width = own_cache.shape[1], own_cache.shape[2]
    cached = own_cache.reshape(2, total_blocks, block_width, heads_here, HEAD_DIM)
    peaks, weight_sums, blended = cache_partials(queries, cached[0], cached[1], cached_count)
    peaks, weight_sums, blended = merge_axis(
        jnp.concatenate([fresh[0][None], peaks]),
        jnp.concatenate([fresh[1][None], weight_sums]),
        jnp.concatenate([fresh[2][None], blended]),
        0,
    )
    attention = (blended / jnp.repeat(weight_sums, HEAD_DIM, axis=-1)).astype(jnp.bfloat16)
    attention = lax.all_to_all(attention, "tp", split_axis=0, concat_axis=1, tiled=True)

    projected = jnp.dot(attention, full_out, preferred_element_type=jnp.float32)
    normed = layer_norm(tokens.astype(jnp.float32) + projected, ln1_gain, ln1_bias).astype(jnp.bfloat16)
    hidden = jax.nn.gelu(
        jnp.dot(normed, full_up, preferred_element_type=jnp.float32) + full_b_up,
        approximate=False,
    ).astype(jnp.bfloat16)
    summed = jnp.dot(hidden, full_down, preferred_element_type=jnp.float32) + b_down + normed.astype(jnp.float32)
    return layer_norm(summed, ln2_gain, ln2_bias).astype(jnp.bfloat16)


def solution(mesh):
    placed = (
        P(("req", "tp"), None),
        P(None, None, "tp"),
        P("tp", None),
        P(None, "tp"),
        P("tp"),
        P("tp", None),
        P(),
        P(),
        P(),
        P(),
        P(),
        P(None, None, "req", "tp"),
        P(),
        P(),
    )
    return jax.shard_map(
        shards, mesh=mesh, in_specs=placed, out_specs=P(("req", "tp"), None), check_vma=False
    )
```

```python
import jax
import jax.numpy as jnp
from jax import lax
from jax.sharding import PartitionSpec as P

HEAD_DIM = 64
BLOCK_GROUP = 4

masked_score = -1e30


def layer_norm(values, gain, bias):
    centre = jnp.mean(values, axis=-1, keepdims=True)
    centred = values - centre
    variance = jnp.mean(centred * centred, axis=-1, keepdims=True)
    return centred * lax.rsqrt(variance + 1e-05) * gain + bias


def partial_attention(queries, key_rows, value_rows, allowed):
    scores = jnp.einsum(
        "chd,nhd->hcn", queries, key_rows, preferred_element_type=jnp.float32
    ) * queries.shape[-1] ** (-0.5)
    scores = jnp.where(allowed[None], scores, masked_score)
    peaks = jnp.max(scores, axis=-1)
    weights = jnp.where(allowed[None], jnp.exp(scores - peaks[..., None]), 0.0).astype(jnp.bfloat16)
    weight_sums = jnp.sum(weights.astype(jnp.float32), axis=-1)
    blended = jnp.einsum("hcn,nhd->chd", weights, value_rows, preferred_element_type=jnp.float32)
    return (peaks.T, weight_sums.T, blended.reshape(blended.shape[0], -1))


def merge_axis(peaks, weight_sums, blended, axis):
    highest = jnp.max(peaks, axis=axis, keepdims=True)
    factors = jnp.exp(peaks - highest)
    sums_out = jnp.sum(factors * weight_sums, axis=axis)
    spread = jnp.repeat(factors, blended.shape[-1] // peaks.shape[-1], axis=-1)
    blend_out = jnp.sum(spread * blended, axis=axis)
    return (jnp.squeeze(highest, axis=axis), sums_out, blend_out)


def cache_partials(queries, keys, values, cached_count):
    total_blocks, block_width = keys.shape[0], keys.shape[1]
    group = BLOCK_GROUP if total_blocks % BLOCK_GROUP == 0 else 1

    def single(one_keys, one_values, block):
        places = block * block_width + jnp.arange(block_width, dtype=jnp.int32)
        allowed = jnp.broadcast_to((places < cached_count)[None, :], (queries.shape[0], block_width))
        return partial_attention(queries, one_keys, one_values, allowed)

    def grouped(items):
        return jax.vmap(single)(*items)

    def regroup(member):
        return member.reshape((total_blocks // group, group) + member.shape[1:])

    results = lax.map(
        grouped,
        (regroup(keys), regroup(values), regroup(jnp.arange(total_blocks, dtype=jnp.int32))),
    )
    return tuple(member.reshape((total_blocks,) + member.shape[2:]) for member in results)


def shards(
    tokens,
    w_qkv,
    w_out,
    w_up,
    b_up,
    w_down,
    b_down,
    ln1_gain,
    ln1_bias,
    ln2_gain,
    ln2_bias,
    kv_cache,
    cache_len,
    span_len,
):
    width_here = w_qkv.shape[2]
    heads_here = width_here // HEAD_DIM
    where_req = lax.axis_index("req")

    own_cache = lax.all_to_all(kv_cache, "req", split_axis=1, concat_axis=1, tiled=True)

    span_rows = lax.all_gather(tokens, "tp", axis=0, tiled=True)
    flat_qkv = w_qkv.reshape(w_qkv.shape[0], 3 * width_here)
    heads_qkv = jnp.dot(span_rows, flat_qkv, preferred_element_type=jnp.float32).astype(jnp.bfloat16)
    span = heads_qkv.shape[0]
    local_shape = (span, heads_here, HEAD_DIM)
    queries = heads_qkv[:, :width_here].reshape(local_shape)
    fresh_keys = heads_qkv[:, width_here : 2 * width_here].reshape(local_shape)
    fresh_values = heads_qkv[:, 2 * width_here :].reshape(local_shape)

    full_out = lax.all_gather(w_out, "tp", axis=0, tiled=True)

    fresh_count = span_len[where_req]
    cached_count = cache_len[where_req]
    positions = jnp.arange(span, dtype=jnp.int32)
    allowed = (positions[None, :] <= positions[:, None]) & (positions[None, :] < fresh_count)
    fresh = partial_attention(queries, fresh_keys, fresh_values, allowed)

    total_blocks, block_width = own_cache.shape[1], own_cache.shape[2]
    cached = own_cache.reshape(2, total_blocks, block_width, heads_here, HEAD_DIM)
    peaks, weight_sums, blended = cache_partials(queries, cached[0], cached[1], cached_count)
    peaks, weight_sums, blended = merge_axis(
        jnp.concatenate([fresh[0][None], peaks]),
        jnp.concatenate([fresh[1][None], weight_sums]),
        jnp.concatenate([fresh[2][None], blended]),
        0,
    )
    attention = (blended / jnp.repeat(weight_sums, HEAD_DIM, axis=-1)).astype(jnp.bfloat16)
    attention = lax.all_to_all(attention, "tp", split_axis=0, concat_axis=1, tiled=True)

    projected = jnp.dot(attention, full_out, preferred_element_type=jnp.float32)
    normed = layer_norm(tokens.astype(jnp.float32) + projected, ln1_gain, ln1_bias).astype(jnp.bfloat16)
    n_tp = lax.axis_size("tp")
    span_normed = lax.all_to_all(
        jnp.broadcast_to(normed[None], (n_tp,) + normed.shape), "tp", split_axis=0, concat_axis=0, tiled=True
    ).reshape(-1, normed.shape[1])
    hidden = jax.nn.gelu(
        jnp.dot(span_normed, w_up, preferred_element_type=jnp.float32) + b_up,
        approximate=False,
    ).astype(jnp.bfloat16)
    partial = jnp.dot(hidden, w_down, preferred_element_type=jnp.float32).astype(jnp.bfloat16)
    partial = lax.all_to_all(
        partial.reshape((n_tp, -1) + partial.shape[1:]), "tp", split_axis=0, concat_axis=0, tiled=True
    )
    summed = jnp.sum(partial.astype(jnp.float32), axis=0) + b_down + normed.astype(jnp.float32)
    return layer_norm(summed, ln2_gain, ln2_bias).astype(jnp.bfloat16)


def solution(mesh):
    placed = (
        P(("req", "tp"), None),
        P(None, None, "tp"),
        P("tp", None),
        P(None, "tp"),
        P("tp"),
        P("tp", None),
        P(),
        P(),
        P(),
        P(),
        P(),
        P(None, None, "req", "tp"),
        P(),
        P(),
    )
    return jax.shard_map(
        shards, mesh=mesh, in_specs=placed, out_specs=P(("req", "tp"), None), check_vma=False
    )
```

```python
import jax
import jax.numpy as jnp
from jax import lax
from jax.experimental import pallas as pl
from jax.experimental.pallas import tpu as pltpu
from jax.sharding import PartitionSpec as P

HEAD_DIM = 64

masked_score = -1e30


def layer_norm(values, gain, bias):
    centre = jnp.mean(values, axis=-1, keepdims=True)
    centred = values - centre
    variance = jnp.mean(centred * centred, axis=-1, keepdims=True)
    return centred * lax.rsqrt(variance + 1e-05) * gain + bias


def partial_attention(queries, key_rows, value_rows, allowed):
    scores = jnp.einsum(
        "chd,nhd->hcn", queries, key_rows, preferred_element_type=jnp.float32
    ) * queries.shape[-1] ** (-0.5)
    scores = jnp.where(allowed[None], scores, masked_score)
    peaks = jnp.max(scores, axis=-1)
    weights = jnp.where(allowed[None], jnp.exp(scores - peaks[..., None]), 0.0).astype(jnp.bfloat16)
    weight_sums = jnp.sum(weights.astype(jnp.float32), axis=-1)
    blended = jnp.einsum("hcn,nhd->chd", weights, value_rows, preferred_element_type=jnp.float32)
    return (peaks.T, weight_sums.T, blended.reshape(blended.shape[0], -1))


def merge_axis(peaks, weight_sums, blended, axis):
    highest = jnp.max(peaks, axis=axis, keepdims=True)
    factors = jnp.exp(peaks - highest)
    sums_out = jnp.sum(factors * weight_sums, axis=axis)
    spread = jnp.repeat(factors, blended.shape[-1] // peaks.shape[-1], axis=-1)
    blend_out = jnp.sum(spread * blended, axis=axis)
    return (jnp.squeeze(highest, axis=axis), sums_out, blend_out)


def cache_kernel(count_ref, q_ref, k_ref, v_ref, acc_ref, peak_ref, sum_ref):
    block = pl.program_id(0)

    @pl.when(block == 0)
    def _():
        acc_ref[...] = jnp.zeros_like(acc_ref)
        peak_ref[...] = jnp.full_like(peak_ref, masked_score)
        sum_ref[...] = jnp.zeros_like(sum_ref)

    width = k_ref.shape[1]
    places = block * width + lax.broadcasted_iota(jnp.int32, (1, width), 1)
    allowed = places < count_ref[0]
    for head in range(peak_ref.shape[0]):
        cols = slice(head * HEAD_DIM, (head + 1) * HEAD_DIM)
        scores = lax.dot_general(
            q_ref[:, cols], k_ref[0, :, cols], (((1,), (1,)), ((), ())), preferred_element_type=jnp.float32
        ) * HEAD_DIM ** (-0.5)
        scores = jnp.where(allowed, scores, masked_score)
        peak = jnp.max(scores, axis=1, keepdims=True)
        weights = jnp.where(allowed, jnp.exp(scores - peak), 0.0).astype(jnp.bfloat16)
        weight_sum = jnp.sum(weights.astype(jnp.float32), axis=1, keepdims=True)
        blend = jnp.dot(weights, v_ref[0, :, cols], preferred_element_type=jnp.float32)
        old = peak_ref[head]
        new = jnp.maximum(old, peak)
        keep = jnp.exp(old - new)
        take = jnp.exp(peak - new)
        peak_ref[head] = new
        sum_ref[head] = sum_ref[head] * keep + weight_sum * take
        acc_ref[:, cols] = acc_ref[:, cols] * keep + blend * take


def cache_partials(queries, own_keys, own_values, cached_count):
    span, width = queries.shape
    total_blocks, block_width = own_keys.shape[0], own_keys.shape[1]
    heads = width // HEAD_DIM
    grid_spec = pltpu.PrefetchScalarGridSpec(
        num_scalar_prefetch=1,
        grid=(total_blocks,),
        in_specs=[
            pl.BlockSpec((span, width), lambda b, c: (0, 0)),
            pl.BlockSpec((1, block_width, width), lambda b, c: (b, 0, 0)),
            pl.BlockSpec((1, block_width, width), lambda b, c: (b, 0, 0)),
        ],
        out_specs=[
            pl.BlockSpec((span, width), lambda b, c: (0, 0)),
            pl.BlockSpec((heads, span, 1), lambda b, c: (0, 0, 0)),
            pl.BlockSpec((heads, span, 1), lambda b, c: (0, 0, 0)),
        ],
    )
    flops = 4 * span * block_width * width * total_blocks
    acc, peaks, sums = pl.pallas_call(
        cache_kernel,
        grid_spec=grid_spec,
        out_shape=[
            jax.ShapeDtypeStruct((span, width), jnp.float32),
            jax.ShapeDtypeStruct((heads, span, 1), jnp.float32),
            jax.ShapeDtypeStruct((heads, span, 1), jnp.float32),
        ],
        compiler_params=pltpu.CompilerParams(dimension_semantics=("arbitrary",)),
        cost_estimate=pl.CostEstimate(
            flops=flops,
            transcendentals=heads * span * block_width * total_blocks,
            bytes_accessed=own_keys.size * 4 + span * width * 6,
        ),
    )(jnp.reshape(cached_count, (1,)), queries, own_keys, own_values)
    return peaks[..., 0].T, sums[..., 0].T, acc


def shards(
    tokens,
    w_qkv,
    w_out,
    w_up,
    b_up,
    w_down,
    b_down,
    ln1_gain,
    ln1_bias,
    ln2_gain,
    ln2_bias,
    kv_cache,
    cache_len,
    span_len,
):
    width_here = w_qkv.shape[2]
    heads_here = width_here // HEAD_DIM
    where_req = lax.axis_index("req")

    own_keys = lax.all_to_all(kv_cache[0], "req", split_axis=0, concat_axis=0, tiled=True)
    own_values = lax.all_to_all(kv_cache[1], "req", split_axis=0, concat_axis=0, tiled=True)

    span_rows = lax.all_gather(tokens, "tp", axis=0, tiled=True)
    flat_qkv = w_qkv.reshape(w_qkv.shape[0], 3 * width_here)
    heads_qkv = jnp.dot(span_rows, flat_qkv, preferred_element_type=jnp.float32).astype(jnp.bfloat16)
    span = heads_qkv.shape[0]
    local_shape = (span, heads_here, HEAD_DIM)
    queries = heads_qkv[:, :width_here].reshape(local_shape)
    fresh_keys = heads_qkv[:, width_here : 2 * width_here].reshape(local_shape)
    fresh_values = heads_qkv[:, 2 * width_here :].reshape(local_shape)

    full_out = lax.all_gather(w_out, "tp", axis=0, tiled=True)

    fresh_count = span_len[where_req]
    cached_count = cache_len[where_req]
    positions = jnp.arange(span, dtype=jnp.int32)
    allowed = (positions[None, :] <= positions[:, None]) & (positions[None, :] < fresh_count)
    fresh = partial_attention(queries, fresh_keys, fresh_values, allowed)

    peaks, weight_sums, blended = cache_partials(heads_qkv[:, :width_here], own_keys, own_values, cached_count)
    peaks, weight_sums, blended = merge_axis(
        jnp.stack([fresh[0], peaks]),
        jnp.stack([fresh[1], weight_sums]),
        jnp.stack([fresh[2], blended]),
        0,
    )
    attention = (blended / jnp.repeat(weight_sums, HEAD_DIM, axis=-1)).astype(jnp.bfloat16)
    attention = lax.all_to_all(attention, "tp", split_axis=0, concat_axis=1, tiled=True)

    projected = jnp.dot(attention, full_out, preferred_element_type=jnp.float32)
    normed = layer_norm(tokens.astype(jnp.float32) + projected, ln1_gain, ln1_bias).astype(jnp.bfloat16)
    n_tp = lax.axis_size("tp")
    span_normed = lax.all_to_all(
        jnp.broadcast_to(normed[None], (n_tp,) + normed.shape), "tp", split_axis=0, concat_axis=0, tiled=True
    ).reshape(-1, normed.shape[1])
    hidden = jax.nn.gelu(
        jnp.dot(span_normed, w_up, preferred_element_type=jnp.float32) + b_up,
        approximate=False,
    ).astype(jnp.bfloat16)
    partial = jnp.dot(hidden, w_down, preferred_element_type=jnp.float32).astype(jnp.bfloat16)
    partial = lax.all_to_all(
        partial.reshape((n_tp, -1) + partial.shape[1:]), "tp", split_axis=0, concat_axis=0, tiled=True
    )
    summed = jnp.sum(partial.astype(jnp.float32), axis=0) + b_down + normed.astype(jnp.float32)
    return layer_norm(summed, ln2_gain, ln2_bias).astype(jnp.bfloat16)


def solution(mesh):
    placed = (
        P(("req", "tp"), None),
        P(None, None, "tp"),
        P("tp", None),
        P(None, "tp"),
        P("tp"),
        P("tp", None),
        P(),
        P(),
        P(),
        P(),
        P(),
        P(None, None, "req", "tp"),
        P(),
        P(),
    )
    return jax.shard_map(
        shards, mesh=mesh, in_specs=placed, out_specs=P(("req", "tp"), None), check_vma=False
    )
```

```python
import jax
import jax.numpy as jnp
from jax import lax
from jax.experimental import pallas as pl
from jax.experimental.pallas import tpu as pltpu
from jax.sharding import PartitionSpec as P

HEAD_DIM = 64

masked_score = -1e30


def layer_norm(values, gain, bias):
    centre = jnp.mean(values, axis=-1, keepdims=True)
    centred = values - centre
    variance = jnp.mean(centred * centred, axis=-1, keepdims=True)
    return centred * lax.rsqrt(variance + 1e-05) * gain + bias


def partial_attention(queries, key_rows, value_rows, allowed):
    scores = jnp.einsum(
        "chd,nhd->hcn", queries, key_rows, preferred_element_type=jnp.float32
    ) * queries.shape[-1] ** (-0.5)
    scores = jnp.where(allowed[None], scores, masked_score)
    peaks = jnp.max(scores, axis=-1)
    weights = jnp.where(allowed[None], jnp.exp(scores - peaks[..., None]), 0.0).astype(jnp.bfloat16)
    weight_sums = jnp.sum(weights.astype(jnp.float32), axis=-1)
    blended = jnp.einsum("hcn,nhd->chd", weights, value_rows, preferred_element_type=jnp.float32)
    return (peaks.T, weight_sums.T, blended.reshape(blended.shape[0], -1))


def merge_axis(peaks, weight_sums, blended, axis):
    highest = jnp.max(peaks, axis=axis, keepdims=True)
    factors = jnp.exp(peaks - highest)
    sums_out = jnp.sum(factors * weight_sums, axis=axis)
    spread = jnp.repeat(factors, blended.shape[-1] // peaks.shape[-1], axis=-1)
    blend_out = jnp.sum(spread * blended, axis=axis)
    return (jnp.squeeze(highest, axis=axis), sums_out, blend_out)


def cache_kernel(count_ref, q_ref, kt_ref, v_ref, acc_ref, peak_ref):
    block = pl.program_id(0)
    heads = q_ref.shape[0]
    width = kt_ref.shape[2]
    start = block * width
    scale = HEAD_DIM ** (-0.5)

    @pl.when(block == 0)
    def _():
        acc_ref[...] = jnp.zeros_like(acc_ref)
        peak_ref[...] = jnp.full_like(peak_ref, masked_score)

    def step(masked):
        allowed = start + lax.broadcasted_iota(jnp.int32, (1, width), 1) < count_ref[0]
        lane = lax.broadcasted_iota(jnp.int32, (1, v_ref.shape[2]), 1)
        for head in range(heads):
            raw = jnp.dot(
                q_ref[head], kt_ref[0, head * HEAD_DIM : (head + 1) * HEAD_DIM, :], preferred_element_type=jnp.float32
            )
            if masked:
                raw = jnp.where(allowed, raw, masked_score)
            top = jnp.max(raw, axis=1, keepdims=True)
            weights = jnp.exp((raw - top) * scale)
            if masked:
                weights = jnp.where(allowed, weights, 0.0)
            weights = weights.astype(jnp.bfloat16)
            own = (lane >= head * HEAD_DIM) & (lane < (head + 1) * HEAD_DIM)
            values = jnp.where(own, v_ref[0], jnp.ones_like(v_ref[0]))
            blend = jnp.dot(weights, values, preferred_element_type=jnp.float32)
            peak = top * scale
            old = peak_ref[head]
            new = jnp.maximum(old, peak)
            peak_ref[head] = new
            acc_ref[head] = acc_ref[head] * jnp.exp(old - new) + blend * jnp.exp(peak - new)

    full = start + width <= count_ref[0]
    some = start < count_ref[0]

    @pl.when(full)
    def _():
        step(False)

    @pl.when(some & jnp.logical_not(full))
    def _():
        step(True)


def cache_partials(queries, own_key_cols, own_values, cached_count):
    span, width = queries.shape
    total_blocks, block_width = own_values.shape[0], own_values.shape[1]
    heads = width // HEAD_DIM
    per_head = queries.reshape(span, heads, HEAD_DIM).transpose(1, 0, 2)
    grid_spec = pltpu.PrefetchScalarGridSpec(
        num_scalar_prefetch=1,
        grid=(total_blocks,),
        in_specs=[
            pl.BlockSpec((heads, span, HEAD_DIM), lambda b, c: (0, 0, 0)),
            pl.BlockSpec((1, width, block_width), lambda b, c: (b, 0, 0)),
            pl.BlockSpec((1, block_width, width), lambda b, c: (b, 0, 0)),
        ],
        out_specs=[
            pl.BlockSpec((heads, span, width), lambda b, c: (0, 0, 0)),
            pl.BlockSpec((heads, span, 1), lambda b, c: (0, 0, 0)),
        ],
    )
    acc, peaks = pl.pallas_call(
        cache_kernel,
        grid_spec=grid_spec,
        out_shape=[
            jax.ShapeDtypeStruct((heads, span, width), jnp.float32),
            jax.ShapeDtypeStruct((heads, span, 1), jnp.float32),
        ],
        compiler_params=pltpu.CompilerParams(dimension_semantics=("arbitrary",)),
        cost_estimate=pl.CostEstimate(
            flops=2 * span * block_width * (HEAD_DIM + width) * heads * total_blocks,
            transcendentals=heads * span * block_width * total_blocks,
            bytes_accessed=own_values.size * 4 + span * width * 2 + heads * span * width * 4,
        ),
    )(jnp.reshape(cached_count, (1,)), per_head, own_key_cols, own_values)
    spare = [((head + 1) % heads) * HEAD_DIM for head in range(heads)]
    blended = jnp.concatenate([acc[head, :, head * HEAD_DIM : (head + 1) * HEAD_DIM] for head in range(heads)], axis=1)
    sums = jnp.stack([acc[head, :, spare[head]] for head in range(heads)], axis=1)
    return peaks[..., 0].T, sums, blended


def shards(
    tokens,
    w_qkv,
    w_out,
    w_up,
    b_up,
    w_down,
    b_down,
    ln1_gain,
    ln1_bias,
    ln2_gain,
    ln2_bias,
    kv_cache,
    cache_len,
    span_len,
):
    width_here = w_qkv.shape[2]
    heads_here = width_here // HEAD_DIM
    where_req = lax.axis_index("req")

    own_key_cols = lax.all_to_all(jnp.swapaxes(kv_cache[0], 1, 2), "req", split_axis=0, concat_axis=0, tiled=True)
    own_values = lax.all_to_all(kv_cache[1], "req", split_axis=0, concat_axis=0, tiled=True)

    span_rows = lax.all_gather(tokens, "tp", axis=0, tiled=True)
    flat_qkv = w_qkv.reshape(w_qkv.shape[0], 3 * width_here)
    heads_qkv = jnp.dot(span_rows, flat_qkv, preferred_element_type=jnp.float32).astype(jnp.bfloat16)
    span = heads_qkv.shape[0]
    local_shape = (span, heads_here, HEAD_DIM)
    queries = heads_qkv[:, :width_here].reshape(local_shape)
    fresh_keys = heads_qkv[:, width_here : 2 * width_here].reshape(local_shape)
    fresh_values = heads_qkv[:, 2 * width_here :].reshape(local_shape)

    full_out = lax.all_gather(w_out, "tp", axis=0, tiled=True)

    fresh_count = span_len[where_req]
    cached_count = cache_len[where_req]
    positions = jnp.arange(span, dtype=jnp.int32)
    allowed = (positions[None, :] <= positions[:, None]) & (positions[None, :] < fresh_count)
    fresh = partial_attention(queries, fresh_keys, fresh_values, allowed)

    peaks, weight_sums, blended = cache_partials(heads_qkv[:, :width_here], own_key_cols, own_values, cached_count)
    peaks, weight_sums, blended = merge_axis(
        jnp.stack([fresh[0], peaks]),
        jnp.stack([fresh[1], weight_sums]),
        jnp.stack([fresh[2], blended]),
        0,
    )
    attention = (blended / jnp.repeat(weight_sums, HEAD_DIM, axis=-1)).astype(jnp.bfloat16)
    attention = lax.all_to_all(attention, "tp", split_axis=0, concat_axis=1, tiled=True)

    projected = jnp.dot(attention, full_out, preferred_element_type=jnp.float32)
    normed = layer_norm(tokens.astype(jnp.float32) + projected, ln1_gain, ln1_bias).astype(jnp.bfloat16)
    n_tp = lax.axis_size("tp")
    span_normed = lax.all_to_all(
        jnp.broadcast_to(normed[None], (n_tp,) + normed.shape), "tp", split_axis=0, concat_axis=0, tiled=True
    ).reshape(-1, normed.shape[1])
    hidden = jax.nn.gelu(
        jnp.dot(span_normed, w_up, preferred_element_type=jnp.float32) + b_up,
        approximate=False,
    ).astype(jnp.bfloat16)
    partial = jnp.dot(hidden, w_down, preferred_element_type=jnp.float32).astype(jnp.bfloat16)
    partial = lax.all_to_all(
        partial.reshape((n_tp, -1) + partial.shape[1:]), "tp", split_axis=0, concat_axis=0, tiled=True
    )
    summed = jnp.sum(partial.astype(jnp.float32), axis=0) + b_down + normed.astype(jnp.float32)
    return layer_norm(summed, ln2_gain, ln2_bias).astype(jnp.bfloat16)


def solution(mesh):
    placed = (
        P(("req", "tp"), None),
        P(None, None, "tp"),
        P("tp", None),
        P(None, "tp"),
        P("tp"),
        P("tp", None),
        P(),
        P(),
        P(),
        P(),
        P(),
        P(None, None, "req", "tp"),
        P(),
        P(),
    )
    return jax.shard_map(
        shards, mesh=mesh, in_specs=placed, out_specs=P(("req", "tp"), None), check_vma=False
    )
```

```python
import functools

import jax
import jax.numpy as jnp
from jax import lax
from jax.experimental import pallas as pl
from jax.experimental.pallas import tpu as pltpu
from jax.sharding import PartitionSpec as P

HEAD_DIM = 64
CHUNKS = 2

masked_score = -1e30


def layer_norm(values, gain, bias):
    centre = jnp.mean(values, axis=-1, keepdims=True)
    centred = values - centre
    variance = jnp.mean(centred * centred, axis=-1, keepdims=True)
    return centred * lax.rsqrt(variance + 1e-05) * gain + bias


def partial_attention(queries, key_rows, value_rows, allowed):
    scores = jnp.einsum(
        "chd,nhd->hcn", queries, key_rows, preferred_element_type=jnp.float32
    ) * queries.shape[-1] ** (-0.5)
    scores = jnp.where(allowed[None], scores, masked_score)
    peaks = jnp.max(scores, axis=-1)
    weights = jnp.where(allowed[None], jnp.exp(scores - peaks[..., None]), 0.0).astype(jnp.bfloat16)
    weight_sums = jnp.sum(weights.astype(jnp.float32), axis=-1)
    blended = jnp.einsum("hcn,nhd->chd", weights, value_rows, preferred_element_type=jnp.float32)
    return (peaks.T, weight_sums.T, blended.reshape(blended.shape[0], -1))


def merge_axis(peaks, weight_sums, blended, axis):
    highest = jnp.max(peaks, axis=axis, keepdims=True)
    factors = jnp.exp(peaks - highest)
    sums_out = jnp.sum(factors * weight_sums, axis=axis)
    spread = jnp.repeat(factors, blended.shape[-1] // peaks.shape[-1], axis=-1)
    blend_out = jnp.sum(spread * blended, axis=axis)
    return (jnp.squeeze(highest, axis=axis), sums_out, blend_out)


def cache_kernel(stride, offset, count_ref, q_ref, kt_ref, v_ref, acc_ref, peak_ref):
    block = pl.program_id(0)
    heads = q_ref.shape[0]
    width = kt_ref.shape[2]
    start = block * stride + offset
    scale = HEAD_DIM ** (-0.5)

    @pl.when(block == 0)
    def _():
        acc_ref[...] = jnp.zeros_like(acc_ref)
        peak_ref[...] = jnp.full_like(peak_ref, masked_score)

    def step(masked):
        allowed = start + lax.broadcasted_iota(jnp.int32, (1, width), 1) < count_ref[0]
        lane = lax.broadcasted_iota(jnp.int32, (1, v_ref.shape[2]), 1)
        for head in range(heads):
            raw = jnp.dot(
                q_ref[head], kt_ref[0, head * HEAD_DIM : (head + 1) * HEAD_DIM, :], preferred_element_type=jnp.float32
            )
            if masked:
                raw = jnp.where(allowed, raw, masked_score)
            top = jnp.max(raw, axis=1, keepdims=True)
            weights = jnp.exp((raw - top) * scale)
            if masked:
                weights = jnp.where(allowed, weights, 0.0)
            weights = weights.astype(jnp.bfloat16)
            own = (lane >= head * HEAD_DIM) & (lane < (head + 1) * HEAD_DIM)
            values = jnp.where(own, v_ref[0], jnp.ones_like(v_ref[0]))
            blend = jnp.dot(weights, values, preferred_element_type=jnp.float32)
            peak = top * scale
            old = peak_ref[head]
            new = jnp.maximum(old, peak)
            peak_ref[head] = new
            acc_ref[head] = acc_ref[head] * jnp.exp(old - new) + blend * jnp.exp(peak - new)

    full = start + width <= count_ref[0]
    some = start < count_ref[0]

    @pl.when(full)
    def _():
        step(False)

    @pl.when(some & jnp.logical_not(full))
    def _():
        step(True)


def cache_partials(queries, own_key_cols, own_values, cached_count, stride, offset):
    span, width = queries.shape
    total_blocks, block_width = own_values.shape[0], own_values.shape[1]
    heads = width // HEAD_DIM
    per_head = queries.reshape(span, heads, HEAD_DIM).transpose(1, 0, 2)
    grid_spec = pltpu.PrefetchScalarGridSpec(
        num_scalar_prefetch=1,
        grid=(total_blocks,),
        in_specs=[
            pl.BlockSpec((heads, span, HEAD_DIM), lambda b, c: (0, 0, 0)),
            pl.BlockSpec((1, width, block_width), lambda b, c: (b, 0, 0)),
            pl.BlockSpec((1, block_width, width), lambda b, c: (b, 0, 0)),
        ],
        out_specs=[
            pl.BlockSpec((heads, span, width), lambda b, c: (0, 0, 0)),
            pl.BlockSpec((heads, span, 1), lambda b, c: (0, 0, 0)),
        ],
    )
    acc, peaks = pl.pallas_call(
        functools.partial(cache_kernel, stride, offset),
        grid_spec=grid_spec,
        out_shape=[
            jax.ShapeDtypeStruct((heads, span, width), jnp.float32),
            jax.ShapeDtypeStruct((heads, span, 1), jnp.float32),
        ],
        compiler_params=pltpu.CompilerParams(dimension_semantics=("arbitrary",)),
        cost_estimate=pl.CostEstimate(
            flops=2 * span * block_width * (HEAD_DIM + width) * heads * total_blocks,
            transcendentals=heads * span * block_width * total_blocks,
            bytes_accessed=own_values.size * 4 + span * width * 2 + heads * span * width * 4,
        ),
    )(jnp.reshape(cached_count, (1,)), per_head, own_key_cols, own_values)
    spare = [((head + 1) % heads) * HEAD_DIM for head in range(heads)]
    blended = jnp.concatenate([acc[head, :, head * HEAD_DIM : (head + 1) * HEAD_DIM] for head in range(heads)], axis=1)
    sums = jnp.stack([acc[head, :, spare[head]] for head in range(heads)], axis=1)
    return peaks[..., 0].T, sums, blended


def shards(
    tokens,
    w_qkv,
    w_out,
    w_up,
    b_up,
    w_down,
    b_down,
    ln1_gain,
    ln1_bias,
    ln2_gain,
    ln2_bias,
    kv_cache,
    cache_len,
    span_len,
):
    width_here = w_qkv.shape[2]
    heads_here = width_here // HEAD_DIM
    where_req = lax.axis_index("req")

    block_len = kv_cache.shape[2]
    chunk_len = block_len // CHUNKS
    moved = []
    for chunk in range(CHUNKS):
        rows = slice(chunk * chunk_len, (chunk + 1) * chunk_len)
        own_values = lax.all_to_all(kv_cache[1][:, rows], "req", split_axis=0, concat_axis=0, tiled=True)
        own_key_cols = lax.all_to_all(
            jnp.swapaxes(kv_cache[0][:, rows], 1, 2), "req", split_axis=0, concat_axis=0, tiled=True
        )
        moved.append((own_key_cols, own_values))

    span_rows = lax.all_gather(tokens, "tp", axis=0, tiled=True)
    flat_qkv = w_qkv.reshape(w_qkv.shape[0], 3 * width_here)
    heads_qkv = jnp.dot(span_rows, flat_qkv, preferred_element_type=jnp.float32).astype(jnp.bfloat16)
    span = heads_qkv.shape[0]
    local_shape = (span, heads_here, HEAD_DIM)
    queries = heads_qkv[:, :width_here].reshape(local_shape)
    fresh_keys = heads_qkv[:, width_here : 2 * width_here].reshape(local_shape)
    fresh_values = heads_qkv[:, 2 * width_here :].reshape(local_shape)

    full_out = lax.all_gather(w_out, "tp", axis=0, tiled=True)

    fresh_count = span_len[where_req]
    cached_count = cache_len[where_req]
    positions = jnp.arange(span, dtype=jnp.int32)
    allowed = (positions[None, :] <= positions[:, None]) & (positions[None, :] < fresh_count)
    fresh = partial_attention(queries, fresh_keys, fresh_values, allowed)

    terms = [fresh] + [
        cache_partials(heads_qkv[:, :width_here], key_cols, values, cached_count, block_len, chunk * chunk_len)
        for chunk, (key_cols, values) in enumerate(moved)
    ]
    peaks, weight_sums, blended = merge_axis(
        jnp.stack([term[0] for term in terms]),
        jnp.stack([term[1] for term in terms]),
        jnp.stack([term[2] for term in terms]),
        0,
    )
    attention = (blended / jnp.repeat(weight_sums, HEAD_DIM, axis=-1)).astype(jnp.bfloat16)
    n_tp = lax.axis_size("tp")
    attention = lax.all_to_all(
        jnp.broadcast_to(attention[None], (n_tp,) + attention.shape), "tp", split_axis=0, concat_axis=2, tiled=True
    ).reshape(span, -1)

    projected = jnp.dot(attention, full_out, preferred_element_type=jnp.float32)
    span_normed = layer_norm(span_rows.astype(jnp.float32) + projected, ln1_gain, ln1_bias).astype(jnp.bfloat16)
    rows_here = tokens.shape[0]
    normed = lax.dynamic_slice_in_dim(span_normed, lax.axis_index("tp") * rows_here, rows_here)
    hidden = jax.nn.gelu(
        jnp.dot(span_normed, w_up, preferred_element_type=jnp.float32) + b_up,
        approximate=False,
    ).astype(jnp.bfloat16)
    partial = jnp.dot(hidden, w_down, preferred_element_type=jnp.float32).astype(jnp.bfloat16)
    partial = lax.all_to_all(
        partial.reshape((n_tp, -1) + partial.shape[1:]), "tp", split_axis=0, concat_axis=0, tiled=True
    )
    summed = jnp.sum(partial.astype(jnp.float32), axis=0) + b_down + normed.astype(jnp.float32)
    return layer_norm(summed, ln2_gain, ln2_bias).astype(jnp.bfloat16)


def solution(mesh):
    placed = (
        P(("req", "tp"), None),
        P(None, None, "tp"),
        P("tp", None),
        P(None, "tp"),
        P("tp"),
        P("tp", None),
        P(),
        P(),
        P(),
        P(),
        P(),
        P(None, None, "req", "tp"),
        P(),
        P(),
    )
    return jax.shard_map(
        shards, mesh=mesh, in_specs=placed, out_specs=P(("req", "tp"), None), check_vma=False
    )
```

```python
import functools

import jax
import jax.numpy as jnp
from jax import lax
from jax.experimental import pallas as pl
from jax.experimental.pallas import tpu as pltpu
from jax.sharding import PartitionSpec as P

HEAD_DIM = 64

masked_score = -1e30


def layer_norm(values, gain, bias):
    centre = jnp.mean(values, axis=-1, keepdims=True)
    centred = values - centre
    variance = jnp.mean(centred * centred, axis=-1, keepdims=True)
    return centred * lax.rsqrt(variance + 1e-05) * gain + bias


def partial_attention(queries, key_rows, value_rows, allowed):
    scores = jnp.einsum(
        "chd,nhd->hcn", queries, key_rows, preferred_element_type=jnp.float32
    ) * queries.shape[-1] ** (-0.5)
    scores = jnp.where(allowed[None], scores, masked_score)
    peaks = jnp.max(scores, axis=-1)
    weights = jnp.where(allowed[None], jnp.exp(scores - peaks[..., None]), 0.0).astype(jnp.bfloat16)
    weight_sums = jnp.sum(weights.astype(jnp.float32), axis=-1)
    blended = jnp.einsum("hcn,nhd->chd", weights, value_rows, preferred_element_type=jnp.float32)
    return (peaks.T, weight_sums.T, blended.reshape(blended.shape[0], -1))


def merge_axis(peaks, weight_sums, blended, axis):
    highest = jnp.max(peaks, axis=axis, keepdims=True)
    factors = jnp.exp(peaks - highest)
    sums_out = jnp.sum(factors * weight_sums, axis=axis)
    spread = jnp.repeat(factors, blended.shape[-1] // peaks.shape[-1], axis=-1)
    blend_out = jnp.sum(spread * blended, axis=axis)
    return (jnp.squeeze(highest, axis=axis), sums_out, blend_out)


def cache_kernel(head, count_ref, q_ref, kt_ref, v_ref, acc_ref, peak_ref):
    block = pl.program_id(0)
    width = kt_ref.shape[2]
    start = block * width
    scale = HEAD_DIM ** (-0.5)

    @pl.when(block == 0)
    def _():
        acc_ref[...] = jnp.zeros_like(acc_ref)
        peak_ref[...] = jnp.full_like(peak_ref, masked_score)

    def step(masked):
        allowed = start + lax.broadcasted_iota(jnp.int32, (1, width), 1) < count_ref[0]
        lane = lax.broadcasted_iota(jnp.int32, (1, v_ref.shape[2]), 1)
        raw = jnp.dot(q_ref[...], kt_ref[0], preferred_element_type=jnp.float32)
        if masked:
            raw = jnp.where(allowed, raw, masked_score)
        top = jnp.max(raw, axis=1, keepdims=True)
        weights = jnp.exp((raw - top) * scale)
        if masked:
            weights = jnp.where(allowed, weights, 0.0)
        weights = weights.astype(jnp.bfloat16)
        own = (lane >= head * HEAD_DIM) & (lane < (head + 1) * HEAD_DIM)
        values = jnp.where(own, v_ref[0], jnp.ones_like(v_ref[0]))
        blend = jnp.dot(weights, values, preferred_element_type=jnp.float32)
        peak = top * scale
        old = peak_ref[...]
        new = jnp.maximum(old, peak)
        peak_ref[...] = new
        acc_ref[...] = acc_ref[...] * jnp.exp(old - new) + blend * jnp.exp(peak - new)

    full = start + width <= count_ref[0]
    some = start < count_ref[0]

    @pl.when(full)
    def _():
        step(False)

    @pl.when(some & jnp.logical_not(full))
    def _():
        step(True)


def cache_partials(head, query, own_key_cols, own_values, cached_count):
    span = query.shape[0]
    total_blocks, block_width, width = own_values.shape
    grid_spec = pltpu.PrefetchScalarGridSpec(
        num_scalar_prefetch=1,
        grid=(total_blocks,),
        in_specs=[
            pl.BlockSpec((span, HEAD_DIM), lambda b, c: (0, 0)),
            pl.BlockSpec((1, HEAD_DIM, block_width), lambda b, c: (b, 0, 0)),
            pl.BlockSpec((1, block_width, width), lambda b, c: (b, 0, 0)),
        ],
        out_specs=[
            pl.BlockSpec((span, width), lambda b, c: (0, 0)),
            pl.BlockSpec((span, 1), lambda b, c: (0, 0)),
        ],
    )
    acc, peak = pl.pallas_call(
        functools.partial(cache_kernel, head),
        grid_spec=grid_spec,
        out_shape=[
            jax.ShapeDtypeStruct((span, width), jnp.float32),
            jax.ShapeDtypeStruct((span, 1), jnp.float32),
        ],
        compiler_params=pltpu.CompilerParams(dimension_semantics=("arbitrary",)),
        cost_estimate=pl.CostEstimate(
            flops=2 * span * block_width * (HEAD_DIM + width) * total_blocks,
            transcendentals=span * block_width * total_blocks,
            bytes_accessed=own_values.size * 3 + span * width * 4,
        ),
    )(jnp.reshape(cached_count, (1,)), query, own_key_cols, own_values)
    spare = ((head + 1) % (width // HEAD_DIM)) * HEAD_DIM
    return peak[:, 0], acc[:, spare], acc[:, head * HEAD_DIM : (head + 1) * HEAD_DIM]


def shards(
    tokens,
    w_qkv,
    w_out,
    w_up,
    b_up,
    w_down,
    b_down,
    ln1_gain,
    ln1_bias,
    ln2_gain,
    ln2_bias,
    kv_cache,
    cache_len,
    span_len,
):
    width_here = w_qkv.shape[2]
    heads_here = width_here // HEAD_DIM
    where_req = lax.axis_index("req")

    own_values = lax.all_to_all(kv_cache[1], "req", split_axis=0, concat_axis=0, tiled=True)
    key_cols = jnp.swapaxes(kv_cache[0], 1, 2)
    own_key_cols = [
        lax.all_to_all(
            key_cols[:, head * HEAD_DIM : (head + 1) * HEAD_DIM], "req", split_axis=0, concat_axis=0, tiled=True
        )
        for head in range(heads_here)
    ]

    span_rows = lax.all_gather(tokens, "tp", axis=0, tiled=True)
    flat_qkv = w_qkv.reshape(w_qkv.shape[0], 3 * width_here)
    heads_qkv = jnp.dot(span_rows, flat_qkv, preferred_element_type=jnp.float32).astype(jnp.bfloat16)
    span = heads_qkv.shape[0]
    local_shape = (span, heads_here, HEAD_DIM)
    queries = heads_qkv[:, :width_here].reshape(local_shape)
    fresh_keys = heads_qkv[:, width_here : 2 * width_here].reshape(local_shape)
    fresh_values = heads_qkv[:, 2 * width_here :].reshape(local_shape)

    full_out = lax.all_gather(w_out, "tp", axis=0, tiled=True)

    fresh_count = span_len[where_req]
    cached_count = cache_len[where_req]
    positions = jnp.arange(span, dtype=jnp.int32)
    allowed = (positions[None, :] <= positions[:, None]) & (positions[None, :] < fresh_count)
    fresh = partial_attention(queries, fresh_keys, fresh_values, allowed)

    per_head = [
        cache_partials(
            head, heads_qkv[:, head * HEAD_DIM : (head + 1) * HEAD_DIM], own_key_cols[head], own_values, cached_count
        )
        for head in range(heads_here)
    ]
    peaks = jnp.stack([term[0] for term in per_head], axis=1)
    weight_sums = jnp.stack([term[1] for term in per_head], axis=1)
    blended = jnp.concatenate([term[2] for term in per_head], axis=1)
    peaks, weight_sums, blended = merge_axis(
        jnp.stack([fresh[0], peaks]),
        jnp.stack([fresh[1], weight_sums]),
        jnp.stack([fresh[2], blended]),
        0,
    )
    attention = (blended / jnp.repeat(weight_sums, HEAD_DIM, axis=-1)).astype(jnp.bfloat16)
    attention = lax.all_to_all(attention, "tp", split_axis=0, concat_axis=1, tiled=True)

    projected = jnp.dot(attention, full_out, preferred_element_type=jnp.float32)
    normed = layer_norm(tokens.astype(jnp.float32) + projected, ln1_gain, ln1_bias).astype(jnp.bfloat16)
    n_tp = lax.axis_size("tp")
    span_normed = lax.all_to_all(
        jnp.broadcast_to(normed[None], (n_tp,) + normed.shape), "tp", split_axis=0, concat_axis=0, tiled=True
    ).reshape(-1, normed.shape[1])
    hidden = jax.nn.gelu(
        jnp.dot(span_normed, w_up, preferred_element_type=jnp.float32) + b_up,
        approximate=False,
    ).astype(jnp.bfloat16)
    partial = jnp.dot(hidden, w_down, preferred_element_type=jnp.float32).astype(jnp.bfloat16)
    partial = lax.all_to_all(
        partial.reshape((n_tp, -1) + partial.shape[1:]), "tp", split_axis=0, concat_axis=0, tiled=True
    )
    summed = jnp.sum(partial.astype(jnp.float32), axis=0) + b_down + normed.astype(jnp.float32)
    return layer_norm(summed, ln2_gain, ln2_bias).astype(jnp.bfloat16)


def solution(mesh):
    placed = (
        P(("req", "tp"), None),
        P(None, None, "tp"),
        P("tp", None),
        P(None, "tp"),
        P("tp"),
        P("tp", None),
        P(),
        P(),
        P(),
        P(),
        P(),
        P(None, None, "req", "tp"),
        P(),
        P(),
    )
    return jax.shard_map(
        shards, mesh=mesh, in_specs=placed, out_specs=P(("req", "tp"), None), check_vma=False
    )
```

```python
import jax
import jax.numpy as jnp
from jax import lax
from jax.experimental import pallas as pl
from jax.experimental.pallas import tpu as pltpu
from jax.sharding import PartitionSpec as P

HEAD_DIM = 64

masked_score = -1e30


def layer_norm(values, gain, bias):
    centre = jnp.mean(values, axis=-1, keepdims=True)
    centred = values - centre
    variance = jnp.mean(centred * centred, axis=-1, keepdims=True)
    return centred * lax.rsqrt(variance + 1e-05) * gain + bias


def partial_attention(queries, key_rows, value_rows, allowed):
    scores = jnp.einsum(
        "chd,nhd->hcn", queries, key_rows, preferred_element_type=jnp.float32
    ) * queries.shape[-1] ** (-0.5)
    scores = jnp.where(allowed[None], scores, masked_score)
    peaks = jnp.max(scores, axis=-1)
    weights = jnp.where(allowed[None], jnp.exp(scores - peaks[..., None]), 0.0).astype(jnp.bfloat16)
    weight_sums = jnp.sum(weights.astype(jnp.float32), axis=-1)
    blended = jnp.einsum("hcn,nhd->chd", weights, value_rows, preferred_element_type=jnp.float32)
    return (peaks.T, weight_sums.T, blended.reshape(blended.shape[0], -1))


def merge_axis(peaks, weight_sums, blended, axis):
    highest = jnp.max(peaks, axis=axis, keepdims=True)
    factors = jnp.exp(peaks - highest)
    sums_out = jnp.sum(factors * weight_sums, axis=axis)
    spread = jnp.repeat(factors, blended.shape[-1] // peaks.shape[-1], axis=-1)
    blend_out = jnp.sum(spread * blended, axis=axis)
    return (jnp.squeeze(highest, axis=axis), sums_out, blend_out)


def score_kernel(count_ref, q_ref, kt_ref, w_ref, peak_ref):
    block = pl.program_id(0)
    heads = q_ref.shape[0]
    width = kt_ref.shape[2]
    start = block * width
    scale = HEAD_DIM ** (-0.5)

    def step(masked):
        allowed = start + lax.broadcasted_iota(jnp.int32, (1, width), 1) < count_ref[0]
        for head in range(heads):
            raw = jnp.dot(
                q_ref[head], kt_ref[0, head * HEAD_DIM : (head + 1) * HEAD_DIM, :], preferred_element_type=jnp.float32
            )
            if masked:
                raw = jnp.where(allowed, raw, masked_score)
            top = jnp.max(raw, axis=1, keepdims=True)
            weights = jnp.exp((raw - top) * scale)
            if masked:
                weights = jnp.where(allowed, weights, 0.0)
            w_ref[0, head] = weights.astype(jnp.bfloat16)
            peak_ref[0, head] = top * scale

    full = start + width <= count_ref[0]
    some = start < count_ref[0]

    @pl.when(full)
    def _():
        step(False)

    @pl.when(some & jnp.logical_not(full))
    def _():
        step(True)

    @pl.when(jnp.logical_not(some))
    def _():
        w_ref[...] = jnp.zeros_like(w_ref)
        peak_ref[...] = jnp.full_like(peak_ref, masked_score)


def blend_kernel(count_ref, w_ref, block_peak_ref, v_ref, acc_ref, peak_ref):
    block = pl.program_id(0)
    heads = w_ref.shape[1]
    width = v_ref.shape[1]
    start = block * width

    @pl.when(block == 0)
    def _():
        acc_ref[...] = jnp.zeros_like(acc_ref)
        peak_ref[...] = jnp.full_like(peak_ref, masked_score)

    @pl.when(start < count_ref[0])
    def _():
        lane = lax.broadcasted_iota(jnp.int32, (1, v_ref.shape[2]), 1)
        for head in range(heads):
            own = (lane >= head * HEAD_DIM) & (lane < (head + 1) * HEAD_DIM)
            values = jnp.where(own, v_ref[0], jnp.ones_like(v_ref[0]))
            blend = jnp.dot(w_ref[0, head], values, preferred_element_type=jnp.float32)
            peak = block_peak_ref[0, head]
            old = peak_ref[head]
            new = jnp.maximum(old, peak)
            peak_ref[head] = new
            acc_ref[head] = acc_ref[head] * jnp.exp(old - new) + blend * jnp.exp(peak - new)


def block_weights(queries, own_key_cols, cached_count):
    span, width = queries.shape
    total_blocks, block_width = own_key_cols.shape[0], own_key_cols.shape[2]
    heads = width // HEAD_DIM
    per_head = queries.reshape(span, heads, HEAD_DIM).transpose(1, 0, 2)
    grid_spec = pltpu.PrefetchScalarGridSpec(
        num_scalar_prefetch=1,
        grid=(total_blocks,),
        in_specs=[
            pl.BlockSpec((heads, span, HEAD_DIM), lambda b, c: (0, 0, 0)),
            pl.BlockSpec((1, width, block_width), lambda b, c: (b, 0, 0)),
        ],
        out_specs=[
            pl.BlockSpec((1, heads, span, block_width), lambda b, c: (b, 0, 0, 0)),
            pl.BlockSpec((1, heads, span, 1), lambda b, c: (b, 0, 0, 0)),
        ],
    )
    return pl.pallas_call(
        score_kernel,
        grid_spec=grid_spec,
        out_shape=[
            jax.ShapeDtypeStruct((total_blocks, heads, span, block_width), jnp.bfloat16),
            jax.ShapeDtypeStruct((total_blocks, heads, span, 1), jnp.float32),
        ],
        compiler_params=pltpu.CompilerParams(dimension_semantics=("arbitrary",)),
        cost_estimate=pl.CostEstimate(
            flops=2 * span * block_width * HEAD_DIM * heads * total_blocks,
            transcendentals=heads * span * block_width * total_blocks,
            bytes_accessed=own_key_cols.size * 2 + total_blocks * heads * span * block_width * 2,
        ),
    )(jnp.reshape(cached_count, (1,)), per_head, own_key_cols)


def cache_partials(weights, block_peaks, own_values, cached_count):
    total_blocks, heads, span, block_width = weights.shape
    width = own_values.shape[2]
    grid_spec = pltpu.PrefetchScalarGridSpec(
        num_scalar_prefetch=1,
        grid=(total_blocks,),
        in_specs=[
            pl.BlockSpec((1, heads, span, block_width), lambda b, c: (b, 0, 0, 0)),
            pl.BlockSpec((1, heads, span, 1), lambda b, c: (b, 0, 0, 0)),
            pl.BlockSpec((1, block_width, width), lambda b, c: (b, 0, 0)),
        ],
        out_specs=[
            pl.BlockSpec((heads, span, width), lambda b, c: (0, 0, 0)),
            pl.BlockSpec((heads, span, 1), lambda b, c: (0, 0, 0)),
        ],
    )
    acc, peaks = pl.pallas_call(
        blend_kernel,
        grid_spec=grid_spec,
        out_shape=[
            jax.ShapeDtypeStruct((heads, span, width), jnp.float32),
            jax.ShapeDtypeStruct((heads, span, 1), jnp.float32),
        ],
        compiler_params=pltpu.CompilerParams(dimension_semantics=("arbitrary",)),
        cost_estimate=pl.CostEstimate(
            flops=2 * span * block_width * width * heads * total_blocks,
            transcendentals=2 * heads * span * total_blocks,
            bytes_accessed=weights.size * 2 + own_values.size * 2 + heads * span * width * 4,
        ),
    )(jnp.reshape(cached_count, (1,)), weights, block_peaks, own_values)
    spare = [((head + 1) % heads) * HEAD_DIM for head in range(heads)]
    blended = jnp.concatenate([acc[head, :, head * HEAD_DIM : (head + 1) * HEAD_DIM] for head in range(heads)], axis=1)
    sums = jnp.stack([acc[head, :, spare[head]] for head in range(heads)], axis=1)
    return peaks[..., 0].T, sums, blended


def shards(
    tokens,
    w_qkv,
    w_out,
    w_up,
    b_up,
    w_down,
    b_down,
    ln1_gain,
    ln1_bias,
    ln2_gain,
    ln2_bias,
    kv_cache,
    cache_len,
    span_len,
):
    width_here = w_qkv.shape[2]
    heads_here = width_here // HEAD_DIM
    where_req = lax.axis_index("req")

    own_key_cols = lax.all_to_all(jnp.swapaxes(kv_cache[0], 1, 2), "req", split_axis=0, concat_axis=0, tiled=True)
    own_key_cols, values_here = lax.optimization_barrier((own_key_cols, kv_cache[1]))
    own_values = lax.all_to_all(values_here, "req", split_axis=0, concat_axis=0, tiled=True)

    span_rows = lax.all_gather(tokens, "tp", axis=0, tiled=True)
    flat_qkv = w_qkv.reshape(w_qkv.shape[0], 3 * width_here)
    heads_qkv = jnp.dot(span_rows, flat_qkv, preferred_element_type=jnp.float32).astype(jnp.bfloat16)
    span = heads_qkv.shape[0]
    local_shape = (span, heads_here, HEAD_DIM)
    queries = heads_qkv[:, :width_here].reshape(local_shape)
    fresh_keys = heads_qkv[:, width_here : 2 * width_here].reshape(local_shape)
    fresh_values = heads_qkv[:, 2 * width_here :].reshape(local_shape)

    full_out = lax.all_gather(w_out, "tp", axis=0, tiled=True)

    fresh_count = span_len[where_req]
    cached_count = cache_len[where_req]
    positions = jnp.arange(span, dtype=jnp.int32)
    allowed = (positions[None, :] <= positions[:, None]) & (positions[None, :] < fresh_count)
    fresh = partial_attention(queries, fresh_keys, fresh_values, allowed)

    weights, block_peaks = block_weights(heads_qkv[:, :width_here], own_key_cols, cached_count)
    peaks, weight_sums, blended = cache_partials(weights, block_peaks, own_values, cached_count)
    peaks, weight_sums, blended = merge_axis(
        jnp.stack([fresh[0], peaks]),
        jnp.stack([fresh[1], weight_sums]),
        jnp.stack([fresh[2], blended]),
        0,
    )
    attention = (blended / jnp.repeat(weight_sums, HEAD_DIM, axis=-1)).astype(jnp.bfloat16)
    attention = lax.all_to_all(attention, "tp", split_axis=0, concat_axis=1, tiled=True)

    projected = jnp.dot(attention, full_out, preferred_element_type=jnp.float32)
    normed = layer_norm(tokens.astype(jnp.float32) + projected, ln1_gain, ln1_bias).astype(jnp.bfloat16)
    n_tp = lax.axis_size("tp")
    span_normed = lax.all_to_all(
        jnp.broadcast_to(normed[None], (n_tp,) + normed.shape), "tp", split_axis=0, concat_axis=0, tiled=True
    ).reshape(-1, normed.shape[1])
    hidden = jax.nn.gelu(
        jnp.dot(span_normed, w_up, preferred_element_type=jnp.float32) + b_up,
        approximate=False,
    ).astype(jnp.bfloat16)
    partial = jnp.dot(hidden, w_down, preferred_element_type=jnp.float32).astype(jnp.bfloat16)
    partial = lax.all_to_all(
        partial.reshape((n_tp, -1) + partial.shape[1:]), "tp", split_axis=0, concat_axis=0, tiled=True
    )
    summed = jnp.sum(partial.astype(jnp.float32), axis=0) + b_down + normed.astype(jnp.float32)
    return layer_norm(summed, ln2_gain, ln2_bias).astype(jnp.bfloat16)


def solution(mesh):
    placed = (
        P(("req", "tp"), None),
        P(None, None, "tp"),
        P("tp", None),
        P(None, "tp"),
        P("tp"),
        P("tp", None),
        P(),
        P(),
        P(),
        P(),
        P(),
        P(None, None, "req", "tp"),
        P(),
        P(),
    )
    return jax.shard_map(
        shards, mesh=mesh, in_specs=placed, out_specs=P(("req", "tp"), None), check_vma=False
    )
```

```python
import jax
import jax.numpy as jnp
from jax import lax
from jax.experimental import pallas as pl
from jax.experimental.pallas import tpu as pltpu
from jax.sharding import PartitionSpec as P

HEAD_DIM = 64

masked_score = -1e30


def layer_norm(values, gain, bias):
    centre = jnp.mean(values, axis=-1, keepdims=True)
    centred = values - centre
    variance = jnp.mean(centred * centred, axis=-1, keepdims=True)
    return centred * lax.rsqrt(variance + 1e-05) * gain + bias


def partial_attention(queries, key_rows, value_rows, allowed):
    scores = jnp.einsum(
        "chd,nhd->hcn", queries, key_rows, preferred_element_type=jnp.float32
    ) * queries.shape[-1] ** (-0.5)
    scores = jnp.where(allowed[None], scores, masked_score)
    peaks = jnp.max(scores, axis=-1)
    weights = jnp.where(allowed[None], jnp.exp(scores - peaks[..., None]), 0.0).astype(jnp.bfloat16)
    weight_sums = jnp.sum(weights.astype(jnp.float32), axis=-1)
    blended = jnp.einsum("hcn,nhd->chd", weights, value_rows, preferred_element_type=jnp.float32)
    return (peaks.T, weight_sums.T, blended.reshape(blended.shape[0], -1))


def merge_axis(peaks, weight_sums, blended, axis):
    highest = jnp.max(peaks, axis=axis, keepdims=True)
    factors = jnp.exp(peaks - highest)
    sums_out = jnp.sum(factors * weight_sums, axis=axis)
    spread = jnp.repeat(factors, blended.shape[-1] // peaks.shape[-1], axis=-1)
    blend_out = jnp.sum(spread * blended, axis=axis)
    return (jnp.squeeze(highest, axis=axis), sums_out, blend_out)


def score_kernel(count_ref, qt_ref, k_ref, w_ref, peak_ref):
    block = pl.program_id(0)
    heads = qt_ref.shape[0]
    width = k_ref.shape[1]
    start = block * width
    scale = HEAD_DIM ** (-0.5)

    def step(masked):
        allowed = start + lax.broadcasted_iota(jnp.int32, (width, 1), 0) < count_ref[0]
        for head in range(heads):
            raw = jnp.dot(k_ref[0], qt_ref[head], preferred_element_type=jnp.float32)
            if masked:
                raw = jnp.where(allowed, raw, masked_score)
            top = jnp.max(raw, axis=0, keepdims=True)
            weights = jnp.exp((raw - top) * scale)
            if masked:
                weights = jnp.where(allowed, weights, 0.0)
            w_ref[0, head] = weights.astype(jnp.bfloat16)
            peak_ref[0, head] = top * scale

    full = start + width <= count_ref[0]
    some = start < count_ref[0]

    @pl.when(full)
    def _():
        step(False)

    @pl.when(some & jnp.logical_not(full))
    def _():
        step(True)

    @pl.when(jnp.logical_not(some))
    def _():
        w_ref[...] = jnp.zeros_like(w_ref)
        peak_ref[...] = jnp.full_like(peak_ref, masked_score)


def blend_kernel(count_ref, w_ref, block_peak_ref, vt_ref, acc_ref, peak_ref):
    block = pl.program_id(0)
    heads = w_ref.shape[1]
    width = vt_ref.shape[2]
    start = block * width

    @pl.when(block == 0)
    def _():
        acc_ref[...] = jnp.zeros_like(acc_ref)
        peak_ref[...] = jnp.full_like(peak_ref, masked_score)

    @pl.when(start < count_ref[0])
    def _():
        row = lax.broadcasted_iota(jnp.int32, (vt_ref.shape[1], 1), 0)
        for head in range(heads):
            own = (row >= head * HEAD_DIM) & (row < (head + 1) * HEAD_DIM)
            values = jnp.where(own, vt_ref[0], jnp.ones_like(vt_ref[0]))
            blend = jnp.dot(values, w_ref[0, head], preferred_element_type=jnp.float32)
            peak = block_peak_ref[0, head]
            old = peak_ref[head]
            new = jnp.maximum(old, peak)
            peak_ref[head] = new
            acc_ref[head] = acc_ref[head] * jnp.exp(old - new) + blend * jnp.exp(peak - new)


def block_weights(queries, own_keys, cached_count):
    span, width = queries.shape
    total_blocks, block_width = own_keys.shape[0], own_keys.shape[1]
    heads = width // HEAD_DIM
    row = jnp.arange(width)[None, :, None] // HEAD_DIM
    padded = jnp.where(row == jnp.arange(heads)[:, None, None], queries.T[None], jnp.zeros_like(queries.T)[None])
    grid_spec = pltpu.PrefetchScalarGridSpec(
        num_scalar_prefetch=1,
        grid=(total_blocks,),
        in_specs=[
            pl.BlockSpec((heads, width, span), lambda b, c: (0, 0, 0)),
            pl.BlockSpec((1, block_width, width), lambda b, c: (b, 0, 0)),
        ],
        out_specs=[
            pl.BlockSpec((1, heads, block_width, span), lambda b, c: (b, 0, 0, 0)),
            pl.BlockSpec((1, heads, 1, span), lambda b, c: (b, 0, 0, 0)),
        ],
    )
    return pl.pallas_call(
        score_kernel,
        grid_spec=grid_spec,
        out_shape=[
            jax.ShapeDtypeStruct((total_blocks, heads, block_width, span), jnp.bfloat16),
            jax.ShapeDtypeStruct((total_blocks, heads, 1, span), jnp.float32),
        ],
        compiler_params=pltpu.CompilerParams(dimension_semantics=("arbitrary",)),
        cost_estimate=pl.CostEstimate(
            flops=2 * span * block_width * width * heads * total_blocks,
            transcendentals=heads * span * block_width * total_blocks,
            bytes_accessed=own_keys.size * 2 + total_blocks * heads * span * block_width * 2,
        ),
    )(jnp.reshape(cached_count, (1,)), padded, own_keys)


def cache_partials(weights, block_peaks, own_value_rows, cached_count):
    total_blocks, heads, block_width, span = weights.shape
    width = own_value_rows.shape[1]
    grid_spec = pltpu.PrefetchScalarGridSpec(
        num_scalar_prefetch=1,
        grid=(total_blocks,),
        in_specs=[
            pl.BlockSpec((1, heads, block_width, span), lambda b, c: (b, 0, 0, 0)),
            pl.BlockSpec((1, heads, 1, span), lambda b, c: (b, 0, 0, 0)),
            pl.BlockSpec((1, width, block_width), lambda b, c: (b, 0, 0)),
        ],
        out_specs=[
            pl.BlockSpec((heads, width, span), lambda b, c: (0, 0, 0)),
            pl.BlockSpec((heads, 1, span), lambda b, c: (0, 0, 0)),
        ],
    )
    acc, peaks = pl.pallas_call(
        blend_kernel,
        grid_spec=grid_spec,
        out_shape=[
            jax.ShapeDtypeStruct((heads, width, span), jnp.float32),
            jax.ShapeDtypeStruct((heads, 1, span), jnp.float32),
        ],
        compiler_params=pltpu.CompilerParams(dimension_semantics=("arbitrary",)),
        cost_estimate=pl.CostEstimate(
            flops=2 * span * block_width * width * heads * total_blocks,
            transcendentals=2 * heads * span * total_blocks,
            bytes_accessed=weights.size * 2 + own_value_rows.size * 2 + heads * span * width * 4,
        ),
    )(jnp.reshape(cached_count, (1,)), weights, block_peaks, own_value_rows)
    spare = [((head + 1) % heads) * HEAD_DIM for head in range(heads)]
    blended = jnp.concatenate([acc[head, head * HEAD_DIM : (head + 1) * HEAD_DIM, :] for head in range(heads)], axis=0).T
    sums = jnp.stack([acc[head, spare[head], :] for head in range(heads)], axis=1)
    return peaks[:, 0, :].T, sums, blended


def shards(
    tokens,
    w_qkv,
    w_out,
    w_up,
    b_up,
    w_down,
    b_down,
    ln1_gain,
    ln1_bias,
    ln2_gain,
    ln2_bias,
    kv_cache,
    cache_len,
    span_len,
):
    width_here = w_qkv.shape[2]
    heads_here = width_here // HEAD_DIM
    where_req = lax.axis_index("req")

    own_keys = lax.all_to_all(kv_cache[0], "req", split_axis=0, concat_axis=0, tiled=True)
    own_keys, value_rows = lax.optimization_barrier((own_keys, jnp.swapaxes(kv_cache[1], 1, 2)))
    own_value_rows = lax.all_to_all(value_rows, "req", split_axis=0, concat_axis=0, tiled=True)

    span_rows = lax.all_gather(tokens, "tp", axis=0, tiled=True)
    flat_qkv = w_qkv.reshape(w_qkv.shape[0], 3 * width_here)
    heads_qkv = jnp.dot(span_rows, flat_qkv, preferred_element_type=jnp.float32).astype(jnp.bfloat16)
    span = heads_qkv.shape[0]
    local_shape = (span, heads_here, HEAD_DIM)
    queries = heads_qkv[:, :width_here].reshape(local_shape)
    fresh_keys = heads_qkv[:, width_here : 2 * width_here].reshape(local_shape)
    fresh_values = heads_qkv[:, 2 * width_here :].reshape(local_shape)

    full_out = lax.all_gather(w_out, "tp", axis=0, tiled=True)

    fresh_count = span_len[where_req]
    cached_count = cache_len[where_req]
    positions = jnp.arange(span, dtype=jnp.int32)
    allowed = (positions[None, :] <= positions[:, None]) & (positions[None, :] < fresh_count)
    fresh = partial_attention(queries, fresh_keys, fresh_values, allowed)

    weights, block_peaks = block_weights(heads_qkv[:, :width_here], own_keys, cached_count)
    peaks, weight_sums, blended = cache_partials(weights, block_peaks, own_value_rows, cached_count)
    peaks, weight_sums, blended = merge_axis(
        jnp.stack([fresh[0], peaks]),
        jnp.stack([fresh[1], weight_sums]),
        jnp.stack([fresh[2], blended]),
        0,
    )
    attention = (blended / jnp.repeat(weight_sums, HEAD_DIM, axis=-1)).astype(jnp.bfloat16)
    attention = lax.all_to_all(attention, "tp", split_axis=0, concat_axis=1, tiled=True)

    projected = jnp.dot(attention, full_out, preferred_element_type=jnp.float32)
    normed = layer_norm(tokens.astype(jnp.float32) + projected, ln1_gain, ln1_bias).astype(jnp.bfloat16)
    n_tp = lax.axis_size("tp")
    span_normed = lax.all_to_all(
        jnp.broadcast_to(normed[None], (n_tp,) + normed.shape), "tp", split_axis=0, concat_axis=0, tiled=True
    ).reshape(-1, normed.shape[1])
    hidden = jax.nn.gelu(
        jnp.dot(span_normed, w_up, preferred_element_type=jnp.float32) + b_up,
        approximate=False,
    ).astype(jnp.bfloat16)
    partial = jnp.dot(hidden, w_down, preferred_element_type=jnp.float32).astype(jnp.bfloat16)
    partial = lax.all_to_all(
        partial.reshape((n_tp, -1) + partial.shape[1:]), "tp", split_axis=0, concat_axis=0, tiled=True
    )
    summed = jnp.sum(partial.astype(jnp.float32), axis=0) + b_down + normed.astype(jnp.float32)
    return layer_norm(summed, ln2_gain, ln2_bias).astype(jnp.bfloat16)


def solution(mesh):
    placed = (
        P(("req", "tp"), None),
        P(None, None, "tp"),
        P("tp", None),
        P(None, "tp"),
        P("tp"),
        P("tp", None),
        P(),
        P(),
        P(),
        P(),
        P(),
        P(None, None, "req", "tp"),
        P(),
        P(),
    )
    return jax.shard_map(
        shards, mesh=mesh, in_specs=placed, out_specs=P(("req", "tp"), None), check_vma=False
    )
```

```python
import jax
import jax.numpy as jnp
from jax import lax
from jax.experimental import pallas as pl
from jax.experimental.pallas import tpu as pltpu
from jax.sharding import PartitionSpec as P

HEAD_DIM = 64
BLEND_STEP = 2

masked_score = -1e30


def layer_norm(values, gain, bias):
    centre = jnp.mean(values, axis=-1, keepdims=True)
    centred = values - centre
    variance = jnp.mean(centred * centred, axis=-1, keepdims=True)
    return centred * lax.rsqrt(variance + 1e-05) * gain + bias


def partial_attention(queries, key_rows, value_rows, allowed):
    scores = jnp.einsum(
        "chd,nhd->hcn", queries, key_rows, preferred_element_type=jnp.float32
    ) * queries.shape[-1] ** (-0.5)
    scores = jnp.where(allowed[None], scores, masked_score)
    peaks = jnp.max(scores, axis=-1)
    weights = jnp.where(allowed[None], jnp.exp(scores - peaks[..., None]), 0.0).astype(jnp.bfloat16)
    weight_sums = jnp.sum(weights.astype(jnp.float32), axis=-1)
    blended = jnp.einsum("hcn,nhd->chd", weights, value_rows, preferred_element_type=jnp.float32)
    return (peaks.T, weight_sums.T, blended.reshape(blended.shape[0], -1))


def merge_axis(peaks, weight_sums, blended, axis):
    highest = jnp.max(peaks, axis=axis, keepdims=True)
    factors = jnp.exp(peaks - highest)
    sums_out = jnp.sum(factors * weight_sums, axis=axis)
    spread = jnp.repeat(factors, blended.shape[-1] // peaks.shape[-1], axis=-1)
    blend_out = jnp.sum(spread * blended, axis=axis)
    return (jnp.squeeze(highest, axis=axis), sums_out, blend_out)


def score_kernel(count_ref, qt_ref, k_ref, w_ref, peak_ref):
    block = pl.program_id(0)
    heads = qt_ref.shape[0]
    width = k_ref.shape[1]
    start = block * width
    scale = HEAD_DIM ** (-0.5)

    def step(masked):
        allowed = start + lax.broadcasted_iota(jnp.int32, (width, 1), 0) < count_ref[0]
        for head in range(heads):
            raw = jnp.dot(k_ref[0], qt_ref[head], preferred_element_type=jnp.float32)
            if masked:
                raw = jnp.where(allowed, raw, masked_score)
            top = jnp.max(raw, axis=0, keepdims=True)
            weights = jnp.exp((raw - top) * scale)
            if masked:
                weights = jnp.where(allowed, weights, 0.0)
            w_ref[0, head] = weights.astype(jnp.bfloat16)
            peak_ref[0, head] = top * scale

    full = start + width <= count_ref[0]
    some = start < count_ref[0]

    @pl.when(full)
    def _():
        step(False)

    @pl.when(some & jnp.logical_not(full))
    def _():
        step(True)

    @pl.when(jnp.logical_not(some))
    def _():
        w_ref[...] = jnp.zeros_like(w_ref)
        peak_ref[...] = jnp.full_like(peak_ref, masked_score)


def blend_kernel(count_ref, w_ref, block_peak_ref, vt_ref, acc_ref, peak_ref):
    step = pl.program_id(0)
    per_step, heads = w_ref.shape[0], w_ref.shape[1]
    width = vt_ref.shape[2]

    @pl.when(step == 0)
    def _():
        acc_ref[...] = jnp.zeros_like(acc_ref)
        peak_ref[...] = jnp.full_like(peak_ref, masked_score)

    for sub in range(per_step):
        start = (step * per_step + sub) * width

        @pl.when(start < count_ref[0])
        def _():
            row = lax.broadcasted_iota(jnp.int32, (vt_ref.shape[1], 1), 0)
            for head in range(heads):
                own = (row >= head * HEAD_DIM) & (row < (head + 1) * HEAD_DIM)
                values = jnp.where(own, vt_ref[sub], jnp.ones_like(vt_ref[sub]))
                blend = jnp.dot(values, w_ref[sub, head], preferred_element_type=jnp.float32)
                peak = block_peak_ref[sub, head]
                old = peak_ref[head]
                new = jnp.maximum(old, peak)
                peak_ref[head] = new
                acc_ref[head] = acc_ref[head] * jnp.exp(old - new) + blend * jnp.exp(peak - new)


def block_weights(queries, own_keys, cached_count):
    span, width = queries.shape
    total_blocks, block_width = own_keys.shape[0], own_keys.shape[1]
    heads = width // HEAD_DIM
    row = jnp.arange(width)[None, :, None] // HEAD_DIM
    padded = jnp.where(row == jnp.arange(heads)[:, None, None], queries.T[None], jnp.zeros_like(queries.T)[None])
    grid_spec = pltpu.PrefetchScalarGridSpec(
        num_scalar_prefetch=1,
        grid=(total_blocks,),
        in_specs=[
            pl.BlockSpec((heads, width, span), lambda b, c: (0, 0, 0)),
            pl.BlockSpec((1, block_width, width), lambda b, c: (b, 0, 0)),
        ],
        out_specs=[
            pl.BlockSpec((1, heads, block_width, span), lambda b, c: (b, 0, 0, 0)),
            pl.BlockSpec((1, heads, 1, span), lambda b, c: (b, 0, 0, 0)),
        ],
    )
    return pl.pallas_call(
        score_kernel,
        grid_spec=grid_spec,
        out_shape=[
            jax.ShapeDtypeStruct((total_blocks, heads, block_width, span), jnp.bfloat16),
            jax.ShapeDtypeStruct((total_blocks, heads, 1, span), jnp.float32),
        ],
        compiler_params=pltpu.CompilerParams(dimension_semantics=("arbitrary",)),
        cost_estimate=pl.CostEstimate(
            flops=2 * span * block_width * width * heads * total_blocks,
            transcendentals=heads * span * block_width * total_blocks,
            bytes_accessed=own_keys.size * 2 + total_blocks * heads * span * block_width * 2,
        ),
    )(jnp.reshape(cached_count, (1,)), padded, own_keys)


def cache_partials(weights, block_peaks, own_value_rows, cached_count):
    total_blocks, heads, block_width, span = weights.shape
    width = own_value_rows.shape[1]
    per_step = BLEND_STEP if total_blocks % BLEND_STEP == 0 else 1
    grid_spec = pltpu.PrefetchScalarGridSpec(
        num_scalar_prefetch=1,
        grid=(total_blocks // per_step,),
        in_specs=[
            pl.BlockSpec((per_step, heads, block_width, span), lambda b, c: (b, 0, 0, 0)),
            pl.BlockSpec((per_step, heads, 1, span), lambda b, c: (b, 0, 0, 0)),
            pl.BlockSpec((per_step, width, block_width), lambda b, c: (b, 0, 0)),
        ],
        out_specs=[
            pl.BlockSpec((heads, width, span), lambda b, c: (0, 0, 0)),
            pl.BlockSpec((heads, 1, span), lambda b, c: (0, 0, 0)),
        ],
    )
    acc, peaks = pl.pallas_call(
        blend_kernel,
        grid_spec=grid_spec,
        out_shape=[
            jax.ShapeDtypeStruct((heads, width, span), jnp.float32),
            jax.ShapeDtypeStruct((heads, 1, span), jnp.float32),
        ],
        compiler_params=pltpu.CompilerParams(dimension_semantics=("arbitrary",)),
        cost_estimate=pl.CostEstimate(
            flops=2 * span * block_width * width * heads * total_blocks,
            transcendentals=2 * heads * span * total_blocks,
            bytes_accessed=weights.size * 2 + own_value_rows.size * 2 + heads * span * width * 4,
        ),
    )(jnp.reshape(cached_count, (1,)), weights, block_peaks, own_value_rows)
    spare = [((head + 1) % heads) * HEAD_DIM for head in range(heads)]
    blended = jnp.concatenate([acc[head, head * HEAD_DIM : (head + 1) * HEAD_DIM, :] for head in range(heads)], axis=0).T
    sums = jnp.stack([acc[head, spare[head], :] for head in range(heads)], axis=1)
    return peaks[:, 0, :].T, sums, blended


def shards(
    tokens,
    w_qkv,
    w_out,
    w_up,
    b_up,
    w_down,
    b_down,
    ln1_gain,
    ln1_bias,
    ln2_gain,
    ln2_bias,
    kv_cache,
    cache_len,
    span_len,
):
    width_here = w_qkv.shape[2]
    heads_here = width_here // HEAD_DIM
    where_req = lax.axis_index("req")

    own_keys = lax.all_to_all(kv_cache[0], "req", split_axis=0, concat_axis=0, tiled=True)
    own_keys, value_rows = lax.optimization_barrier((own_keys, jnp.swapaxes(kv_cache[1], 1, 2)))
    own_value_rows = lax.all_to_all(value_rows, "req", split_axis=0, concat_axis=0, tiled=True)

    span_rows = lax.all_gather(tokens, "tp", axis=0, tiled=True)
    flat_qkv = w_qkv.reshape(w_qkv.shape[0], 3 * width_here)
    heads_qkv = jnp.dot(span_rows, flat_qkv, preferred_element_type=jnp.float32).astype(jnp.bfloat16)
    span = heads_qkv.shape[0]
    local_shape = (span, heads_here, HEAD_DIM)
    queries = heads_qkv[:, :width_here].reshape(local_shape)
    fresh_keys = heads_qkv[:, width_here : 2 * width_here].reshape(local_shape)
    fresh_values = heads_qkv[:, 2 * width_here :].reshape(local_shape)

    full_out = lax.all_gather(w_out, "tp", axis=0, tiled=True)

    fresh_count = span_len[where_req]
    cached_count = cache_len[where_req]
    positions = jnp.arange(span, dtype=jnp.int32)
    allowed = (positions[None, :] <= positions[:, None]) & (positions[None, :] < fresh_count)
    fresh = partial_attention(queries, fresh_keys, fresh_values, allowed)

    weights, block_peaks = block_weights(heads_qkv[:, :width_here], own_keys, cached_count)
    peaks, weight_sums, blended = cache_partials(weights, block_peaks, own_value_rows, cached_count)
    peaks, weight_sums, blended = merge_axis(
        jnp.stack([fresh[0], peaks]),
        jnp.stack([fresh[1], weight_sums]),
        jnp.stack([fresh[2], blended]),
        0,
    )
    attention = (blended / jnp.repeat(weight_sums, HEAD_DIM, axis=-1)).astype(jnp.bfloat16)
    attention = lax.all_to_all(attention, "tp", split_axis=0, concat_axis=1, tiled=True)

    projected = jnp.dot(attention, full_out, preferred_element_type=jnp.float32)
    normed = layer_norm(tokens.astype(jnp.float32) + projected, ln1_gain, ln1_bias).astype(jnp.bfloat16)
    n_tp = lax.axis_size("tp")
    span_normed = lax.all_to_all(
        jnp.broadcast_to(normed[None], (n_tp,) + normed.shape), "tp", split_axis=0, concat_axis=0, tiled=True
    ).reshape(-1, normed.shape[1])
    hidden = jax.nn.gelu(
        jnp.dot(span_normed, w_up, preferred_element_type=jnp.float32) + b_up,
        approximate=False,
    ).astype(jnp.bfloat16)
    partial = jnp.dot(hidden, w_down, preferred_element_type=jnp.float32).astype(jnp.bfloat16)
    partial = lax.all_to_all(
        partial.reshape((n_tp, -1) + partial.shape[1:]), "tp", split_axis=0, concat_axis=0, tiled=True
    )
    summed = jnp.sum(partial.astype(jnp.float32), axis=0) + b_down + normed.astype(jnp.float32)
    return layer_norm(summed, ln2_gain, ln2_bias).astype(jnp.bfloat16)


def solution(mesh):
    placed = (
        P(("req", "tp"), None),
        P(None, None, "tp"),
        P("tp", None),
        P(None, "tp"),
        P("tp"),
        P("tp", None),
        P(),
        P(),
        P(),
        P(),
        P(),
        P(None, None, "req", "tp"),
        P(),
        P(),
    )
    return jax.shard_map(
        shards, mesh=mesh, in_specs=placed, out_specs=P(("req", "tp"), None), check_vma=False
    )
```

```python
import jax
import jax.numpy as jnp
from jax import lax
from jax.experimental import pallas as pl
from jax.experimental.pallas import tpu as pltpu
from jax.sharding import PartitionSpec as P

HEAD_DIM = 64
BLEND_STEP = 4

masked_score = -1e30


def layer_norm(values, gain, bias):
    centre = jnp.mean(values, axis=-1, keepdims=True)
    centred = values - centre
    variance = jnp.mean(centred * centred, axis=-1, keepdims=True)
    return centred * lax.rsqrt(variance + 1e-05) * gain + bias


def partial_attention(queries, key_rows, value_rows, allowed):
    scores = jnp.einsum(
        "chd,nhd->hcn", queries, key_rows, preferred_element_type=jnp.float32
    ) * queries.shape[-1] ** (-0.5)
    scores = jnp.where(allowed[None], scores, masked_score)
    peaks = jnp.max(scores, axis=-1)
    weights = jnp.where(allowed[None], jnp.exp(scores - peaks[..., None]), 0.0).astype(jnp.bfloat16)
    weight_sums = jnp.sum(weights.astype(jnp.float32), axis=-1)
    blended = jnp.einsum("hcn,nhd->chd", weights, value_rows, preferred_element_type=jnp.float32)
    return (peaks.T, weight_sums.T, blended.reshape(blended.shape[0], -1))


def merge_axis(peaks, weight_sums, blended, axis):
    highest = jnp.max(peaks, axis=axis, keepdims=True)
    factors = jnp.exp(peaks - highest)
    sums_out = jnp.sum(factors * weight_sums, axis=axis)
    spread = jnp.repeat(factors, blended.shape[-1] // peaks.shape[-1], axis=-1)
    blend_out = jnp.sum(spread * blended, axis=axis)
    return (jnp.squeeze(highest, axis=axis), sums_out, blend_out)


def score_kernel(count_ref, qt_ref, k_ref, w_ref, peak_ref):
    block = pl.program_id(0)
    heads = qt_ref.shape[0]
    width = k_ref.shape[1]
    start = block * width
    scale = HEAD_DIM ** (-0.5)

    def step(masked):
        allowed = start + lax.broadcasted_iota(jnp.int32, (width, 1), 0) < count_ref[0]
        for head in range(heads):
            raw = jnp.dot(k_ref[0], qt_ref[head], preferred_element_type=jnp.float32)
            if masked:
                raw = jnp.where(allowed, raw, masked_score)
            top = jnp.max(raw, axis=0, keepdims=True)
            weights = jnp.exp((raw - top) * scale)
            if masked:
                weights = jnp.where(allowed, weights, 0.0)
            w_ref[0, head] = weights.astype(jnp.bfloat16)
            peak_ref[0, head] = top * scale

    full = start + width <= count_ref[0]
    some = start < count_ref[0]

    @pl.when(full)
    def _():
        step(False)

    @pl.when(some & jnp.logical_not(full))
    def _():
        step(True)

    @pl.when(jnp.logical_not(some))
    def _():
        w_ref[...] = jnp.zeros_like(w_ref)
        peak_ref[...] = jnp.full_like(peak_ref, masked_score)


def blend_kernel(count_ref, w_ref, block_peak_ref, vt_ref, acc_ref, peak_ref):
    step = pl.program_id(0)
    per_step, heads = w_ref.shape[0], w_ref.shape[1]
    width = vt_ref.shape[2]

    @pl.when(step == 0)
    def _():
        acc_ref[...] = jnp.zeros_like(acc_ref)
        peak_ref[...] = jnp.full_like(peak_ref, masked_score)

    for sub in range(per_step):
        start = (step * per_step + sub) * width

        @pl.when(start < count_ref[0])
        def _():
            row = lax.broadcasted_iota(jnp.int32, (vt_ref.shape[1], 1), 0)
            for head in range(heads):
                own = (row >= head * HEAD_DIM) & (row < (head + 1) * HEAD_DIM)
                values = jnp.where(own, vt_ref[sub], jnp.ones_like(vt_ref[sub]))
                blend = jnp.dot(values, w_ref[sub, head], preferred_element_type=jnp.float32)
                peak = block_peak_ref[sub, head]
                old = peak_ref[head]
                new = jnp.maximum(old, peak)
                peak_ref[head] = new
                acc_ref[head] = acc_ref[head] * jnp.exp(old - new) + blend * jnp.exp(peak - new)


def block_weights(queries, own_keys, cached_count):
    span, width = queries.shape
    total_blocks, block_width = own_keys.shape[0], own_keys.shape[1]
    heads = width // HEAD_DIM
    row = jnp.arange(width)[None, :, None] // HEAD_DIM
    padded = jnp.where(row == jnp.arange(heads)[:, None, None], queries.T[None], jnp.zeros_like(queries.T)[None])
    grid_spec = pltpu.PrefetchScalarGridSpec(
        num_scalar_prefetch=1,
        grid=(total_blocks,),
        in_specs=[
            pl.BlockSpec((heads, width, span), lambda b, c: (0, 0, 0)),
            pl.BlockSpec((1, block_width, width), lambda b, c: (b, 0, 0)),
        ],
        out_specs=[
            pl.BlockSpec((1, heads, block_width, span), lambda b, c: (b, 0, 0, 0)),
            pl.BlockSpec((1, heads, 1, span), lambda b, c: (b, 0, 0, 0)),
        ],
    )
    return pl.pallas_call(
        score_kernel,
        grid_spec=grid_spec,
        out_shape=[
            jax.ShapeDtypeStruct((total_blocks, heads, block_width, span), jnp.bfloat16),
            jax.ShapeDtypeStruct((total_blocks, heads, 1, span), jnp.float32),
        ],
        compiler_params=pltpu.CompilerParams(dimension_semantics=("arbitrary",)),
        cost_estimate=pl.CostEstimate(
            flops=2 * span * block_width * width * heads * total_blocks,
            transcendentals=heads * span * block_width * total_blocks,
            bytes_accessed=own_keys.size * 2 + total_blocks * heads * span * block_width * 2,
        ),
    )(jnp.reshape(cached_count, (1,)), padded, own_keys)


def cache_partials(weights, block_peaks, own_value_rows, cached_count):
    total_blocks, heads, block_width, span = weights.shape
    width = own_value_rows.shape[1]
    per_step = BLEND_STEP if total_blocks % BLEND_STEP == 0 else 1
    grid_spec = pltpu.PrefetchScalarGridSpec(
        num_scalar_prefetch=1,
        grid=(total_blocks // per_step,),
        in_specs=[
            pl.BlockSpec((per_step, heads, block_width, span), lambda b, c: (b, 0, 0, 0)),
            pl.BlockSpec((per_step, heads, 1, span), lambda b, c: (b, 0, 0, 0)),
            pl.BlockSpec((per_step, width, block_width), lambda b, c: (b, 0, 0)),
        ],
        out_specs=[
            pl.BlockSpec((heads, width, span), lambda b, c: (0, 0, 0)),
            pl.BlockSpec((heads, 1, span), lambda b, c: (0, 0, 0)),
        ],
    )
    acc, peaks = pl.pallas_call(
        blend_kernel,
        grid_spec=grid_spec,
        out_shape=[
            jax.ShapeDtypeStruct((heads, width, span), jnp.float32),
            jax.ShapeDtypeStruct((heads, 1, span), jnp.float32),
        ],
        compiler_params=pltpu.CompilerParams(dimension_semantics=("arbitrary",)),
        cost_estimate=pl.CostEstimate(
            flops=2 * span * block_width * width * heads * total_blocks,
            transcendentals=2 * heads * span * total_blocks,
            bytes_accessed=weights.size * 2 + own_value_rows.size * 2 + heads * span * width * 4,
        ),
    )(jnp.reshape(cached_count, (1,)), weights, block_peaks, own_value_rows)
    spare = [((head + 1) % heads) * HEAD_DIM for head in range(heads)]
    blended = jnp.concatenate([acc[head, head * HEAD_DIM : (head + 1) * HEAD_DIM, :] for head in range(heads)], axis=0).T
    sums = jnp.stack([acc[head, spare[head], :] for head in range(heads)], axis=1)
    return peaks[:, 0, :].T, sums, blended


def shards(
    tokens,
    w_qkv,
    w_out,
    w_up,
    b_up,
    w_down,
    b_down,
    ln1_gain,
    ln1_bias,
    ln2_gain,
    ln2_bias,
    kv_cache,
    cache_len,
    span_len,
):
    width_here = w_qkv.shape[2]
    heads_here = width_here // HEAD_DIM
    where_req = lax.axis_index("req")

    own_keys = lax.all_to_all(kv_cache[0], "req", split_axis=0, concat_axis=0, tiled=True)
    own_keys, value_rows = lax.optimization_barrier((own_keys, jnp.swapaxes(kv_cache[1], 1, 2)))
    own_value_rows = lax.all_to_all(value_rows, "req", split_axis=0, concat_axis=0, tiled=True)

    span_rows = lax.all_gather(tokens, "tp", axis=0, tiled=True)
    flat_qkv = w_qkv.reshape(w_qkv.shape[0], 3 * width_here)
    heads_qkv = jnp.dot(span_rows, flat_qkv, preferred_element_type=jnp.float32).astype(jnp.bfloat16)
    span = heads_qkv.shape[0]
    local_shape = (span, heads_here, HEAD_DIM)
    queries = heads_qkv[:, :width_here].reshape(local_shape)
    fresh_keys = heads_qkv[:, width_here : 2 * width_here].reshape(local_shape)
    fresh_values = heads_qkv[:, 2 * width_here :].reshape(local_shape)

    full_out = lax.all_gather(w_out, "tp", axis=0, tiled=True)

    fresh_count = span_len[where_req]
    cached_count = cache_len[where_req]
    positions = jnp.arange(span, dtype=jnp.int32)
    allowed = (positions[None, :] <= positions[:, None]) & (positions[None, :] < fresh_count)
    fresh = partial_attention(queries, fresh_keys, fresh_values, allowed)

    weights, block_peaks = block_weights(heads_qkv[:, :width_here], own_keys, cached_count)
    peaks, weight_sums, blended = cache_partials(weights, block_peaks, own_value_rows, cached_count)
    peaks, weight_sums, blended = merge_axis(
        jnp.stack([fresh[0], peaks]),
        jnp.stack([fresh[1], weight_sums]),
        jnp.stack([fresh[2], blended]),
        0,
    )
    attention = (blended / jnp.repeat(weight_sums, HEAD_DIM, axis=-1)).astype(jnp.bfloat16)
    attention = lax.all_to_all(attention, "tp", split_axis=0, concat_axis=1, tiled=True)

    projected = jnp.dot(attention, full_out, preferred_element_type=jnp.float32)
    normed = layer_norm(tokens.astype(jnp.float32) + projected, ln1_gain, ln1_bias).astype(jnp.bfloat16)
    n_tp = lax.axis_size("tp")
    span_normed = lax.all_to_all(
        jnp.broadcast_to(normed[None], (n_tp,) + normed.shape), "tp", split_axis=0, concat_axis=0, tiled=True
    ).reshape(-1, normed.shape[1])
    hidden = jax.nn.gelu(
        jnp.dot(span_normed, w_up, preferred_element_type=jnp.float32) + b_up,
        approximate=False,
    ).astype(jnp.bfloat16)
    partial = jnp.dot(hidden, w_down, preferred_element_type=jnp.float32).astype(jnp.bfloat16)
    partial = lax.all_to_all(
        partial.reshape((n_tp, -1) + partial.shape[1:]), "tp", split_axis=0, concat_axis=0, tiled=True
    )
    summed = jnp.sum(partial.astype(jnp.float32), axis=0) + b_down + normed.astype(jnp.float32)
    return layer_norm(summed, ln2_gain, ln2_bias).astype(jnp.bfloat16)


def solution(mesh):
    placed = (
        P(("req", "tp"), None),
        P(None, None, "tp"),
        P("tp", None),
        P(None, "tp"),
        P("tp"),
        P("tp", None),
        P(),
        P(),
        P(),
        P(),
        P(),
        P(None, None, "req", "tp"),
        P(),
        P(),
    )
    return jax.shard_map(
        shards, mesh=mesh, in_specs=placed, out_specs=P(("req", "tp"), None), check_vma=False
    )
```

```python
import jax
import jax.numpy as jnp
from jax import lax
from jax.experimental import pallas as pl
from jax.experimental.pallas import tpu as pltpu
from jax.sharding import PartitionSpec as P

HEAD_DIM = 64
BLEND_STEP = 4

masked_score = -1e30


def layer_norm(values, gain, bias):
    centre = jnp.mean(values, axis=-1, keepdims=True)
    centred = values - centre
    variance = jnp.mean(centred * centred, axis=-1, keepdims=True)
    return centred * lax.rsqrt(variance + 1e-05) * gain + bias


def partial_attention(queries, key_rows, value_rows, allowed):
    scores = jnp.einsum(
        "chd,nhd->hcn", queries, key_rows, preferred_element_type=jnp.float32
    ) * queries.shape[-1] ** (-0.5)
    scores = jnp.where(allowed[None], scores, masked_score)
    peaks = jnp.max(scores, axis=-1)
    weights = jnp.where(allowed[None], jnp.exp(scores - peaks[..., None]), 0.0).astype(jnp.bfloat16)
    weight_sums = jnp.sum(weights.astype(jnp.float32), axis=-1)
    blended = jnp.einsum("hcn,nhd->chd", weights, value_rows, preferred_element_type=jnp.float32)
    return (peaks.T, weight_sums.T, blended.reshape(blended.shape[0], -1))


def merge_axis(peaks, weight_sums, blended, axis):
    highest = jnp.max(peaks, axis=axis, keepdims=True)
    factors = jnp.exp(peaks - highest)
    sums_out = jnp.sum(factors * weight_sums, axis=axis)
    spread = jnp.repeat(factors, blended.shape[-1] // peaks.shape[-1], axis=-1)
    blend_out = jnp.sum(spread * blended, axis=axis)
    return (jnp.squeeze(highest, axis=axis), sums_out, blend_out)


def score_kernel(count_ref, qt_ref, k_ref, w_ref, peak_ref):
    block = pl.program_id(0)
    heads = qt_ref.shape[0]
    width = k_ref.shape[1]
    start = block * width
    scale = HEAD_DIM ** (-0.5)

    def step(masked):
        allowed = start + lax.broadcasted_iota(jnp.int32, (width, 1), 0) < count_ref[0]
        for head in range(heads):
            raw = jnp.dot(k_ref[0], qt_ref[head], preferred_element_type=jnp.float32)
            if masked:
                raw = jnp.where(allowed, raw, masked_score)
            top = jnp.max(raw, axis=0, keepdims=True)
            weights = jnp.exp((raw - top) * scale)
            if masked:
                weights = jnp.where(allowed, weights, 0.0)
            w_ref[0, head] = weights.astype(jnp.bfloat16)
            peak_ref[0, head] = top * scale

    full = start + width <= count_ref[0]
    some = start < count_ref[0]

    @pl.when(full)
    def _():
        step(False)

    @pl.when(some & jnp.logical_not(full))
    def _():
        step(True)

    @pl.when(jnp.logical_not(some))
    def _():
        w_ref[...] = jnp.zeros_like(w_ref)
        peak_ref[...] = jnp.full_like(peak_ref, masked_score)


def blend_kernel(count_ref, w_ref, block_peak_ref, vt_ref, acc_ref, peak_ref):
    step = pl.program_id(0)
    per_step, heads = w_ref.shape[0], w_ref.shape[1]
    width = vt_ref.shape[2]

    @pl.when(step == 0)
    def _():
        acc_ref[...] = jnp.zeros_like(acc_ref)
        peak_ref[...] = jnp.full_like(peak_ref, masked_score)

    for sub in range(per_step):
        start = (step * per_step + sub) * width

        @pl.when(start < count_ref[0])
        def _():
            row = lax.broadcasted_iota(jnp.int32, (vt_ref.shape[1], 1), 0)
            for head in range(heads):
                own = (row >= head * HEAD_DIM) & (row < (head + 1) * HEAD_DIM)
                values = jnp.where(own, vt_ref[sub], jnp.ones_like(vt_ref[sub]))
                blend = jnp.dot(values, w_ref[sub, head], preferred_element_type=jnp.float32)
                peak = block_peak_ref[sub, head]
                old = peak_ref[head]
                new = jnp.maximum(old, peak)
                peak_ref[head] = new
                acc_ref[head] = acc_ref[head] * jnp.exp(old - new) + blend * jnp.exp(peak - new)


def block_weights(queries, own_keys, cached_count):
    span, width = queries.shape
    total_blocks, block_width = own_keys.shape[0], own_keys.shape[1]
    heads = width // HEAD_DIM
    row = jnp.arange(width)[None, :, None] // HEAD_DIM
    padded = jnp.where(row == jnp.arange(heads)[:, None, None], queries.T[None], jnp.zeros_like(queries.T)[None])
    grid_spec = pltpu.PrefetchScalarGridSpec(
        num_scalar_prefetch=1,
        grid=(total_blocks,),
        in_specs=[
            pl.BlockSpec((heads, width, span), lambda b, c: (0, 0, 0)),
            pl.BlockSpec((1, block_width, width), lambda b, c: (b, 0, 0)),
        ],
        out_specs=[
            pl.BlockSpec((1, heads, block_width, span), lambda b, c: (b, 0, 0, 0)),
            pl.BlockSpec((1, heads, 1, span), lambda b, c: (b, 0, 0, 0)),
        ],
    )
    return pl.pallas_call(
        score_kernel,
        grid_spec=grid_spec,
        out_shape=[
            jax.ShapeDtypeStruct((total_blocks, heads, block_width, span), jnp.bfloat16),
            jax.ShapeDtypeStruct((total_blocks, heads, 1, span), jnp.float32),
        ],
        compiler_params=pltpu.CompilerParams(dimension_semantics=("arbitrary",)),
        cost_estimate=pl.CostEstimate(
            flops=2 * span * block_width * width * heads * total_blocks,
            transcendentals=heads * span * block_width * total_blocks,
            bytes_accessed=own_keys.size * 2 + total_blocks * heads * span * block_width * 2,
        ),
    )(jnp.reshape(cached_count, (1,)), padded, own_keys)


def cache_partials(weights, block_peaks, own_value_rows, cached_count):
    total_blocks, heads, block_width, span = weights.shape
    width = own_value_rows.shape[1]
    per_step = BLEND_STEP if total_blocks % BLEND_STEP == 0 else 1
    grid_spec = pltpu.PrefetchScalarGridSpec(
        num_scalar_prefetch=1,
        grid=(total_blocks // per_step,),
        in_specs=[
            pl.BlockSpec((per_step, heads, block_width, span), lambda b, c: (b, 0, 0, 0)),
            pl.BlockSpec((per_step, heads, 1, span), lambda b, c: (b, 0, 0, 0)),
            pl.BlockSpec((per_step, width, block_width), lambda b, c: (b, 0, 0)),
        ],
        out_specs=[
            pl.BlockSpec((heads, width, span), lambda b, c: (0, 0, 0)),
            pl.BlockSpec((heads, 1, span), lambda b, c: (0, 0, 0)),
        ],
    )
    acc, peaks = pl.pallas_call(
        blend_kernel,
        grid_spec=grid_spec,
        out_shape=[
            jax.ShapeDtypeStruct((heads, width, span), jnp.float32),
            jax.ShapeDtypeStruct((heads, 1, span), jnp.float32),
        ],
        compiler_params=pltpu.CompilerParams(dimension_semantics=("arbitrary",)),
        cost_estimate=pl.CostEstimate(
            flops=2 * span * block_width * width * heads * total_blocks,
            transcendentals=2 * heads * span * total_blocks,
            bytes_accessed=weights.size * 2 + own_value_rows.size * 2 + heads * span * width * 4,
        ),
    )(jnp.reshape(cached_count, (1,)), weights, block_peaks, own_value_rows)
    spare = [((head + 1) % heads) * HEAD_DIM for head in range(heads)]
    blended = jnp.concatenate([acc[head, head * HEAD_DIM : (head + 1) * HEAD_DIM, :] for head in range(heads)], axis=0).T
    sums = jnp.stack([acc[head, spare[head], :] for head in range(heads)], axis=1)
    return peaks[:, 0, :].T, sums, blended


def shards(
    tokens,
    w_qkv,
    w_out,
    w_up,
    b_up,
    w_down,
    b_down,
    ln1_gain,
    ln1_bias,
    ln2_gain,
    ln2_bias,
    kv_cache,
    cache_len,
    span_len,
):
    width_here = w_qkv.shape[2]
    heads_here = width_here // HEAD_DIM
    where_req = lax.axis_index("req")

    own_keys = lax.all_to_all(kv_cache[0], "req", split_axis=0, concat_axis=0, tiled=True)
    own_keys, value_rows = lax.optimization_barrier((own_keys, jnp.swapaxes(kv_cache[1], 1, 2)))
    own_value_rows = lax.all_to_all(value_rows, "req", split_axis=0, concat_axis=0, tiled=True)

    span_rows = lax.all_gather(tokens, "tp", axis=0, tiled=True)
    flat_qkv = w_qkv.reshape(w_qkv.shape[0], 3 * width_here)
    heads_qkv = jnp.dot(span_rows, flat_qkv, preferred_element_type=jnp.float32).astype(jnp.bfloat16)
    span = heads_qkv.shape[0]
    local_shape = (span, heads_here, HEAD_DIM)
    queries = heads_qkv[:, :width_here].reshape(local_shape)
    fresh_keys = heads_qkv[:, width_here : 2 * width_here].reshape(local_shape)
    fresh_values = heads_qkv[:, 2 * width_here :].reshape(local_shape)

    full_out = lax.all_gather(w_out, "tp", axis=0, tiled=True)

    fresh_count = span_len[where_req]
    cached_count = cache_len[where_req]
    positions = jnp.arange(span, dtype=jnp.int32)
    allowed = (positions[None, :] <= positions[:, None]) & (positions[None, :] < fresh_count)
    fresh = partial_attention(queries, fresh_keys, fresh_values, allowed)

    weights, block_peaks = block_weights(heads_qkv[:, :width_here], own_keys, cached_count)
    peaks, weight_sums, blended = cache_partials(weights, block_peaks, own_value_rows, cached_count)
    peaks, weight_sums, blended = merge_axis(
        jnp.stack([fresh[0], peaks]),
        jnp.stack([fresh[1], weight_sums]),
        jnp.stack([fresh[2], blended]),
        0,
    )
    attention = (blended / jnp.repeat(weight_sums, HEAD_DIM, axis=-1)).astype(jnp.bfloat16)
    n_tp = lax.axis_size("tp")
    attention = lax.all_to_all(
        jnp.broadcast_to(attention[None], (n_tp,) + attention.shape), "tp", split_axis=0, concat_axis=2, tiled=True
    ).reshape(span, -1)

    projected = jnp.dot(attention, full_out, preferred_element_type=jnp.float32)
    span_normed = layer_norm(span_rows.astype(jnp.float32) + projected, ln1_gain, ln1_bias).astype(jnp.bfloat16)
    rows_here = tokens.shape[0]
    normed = lax.dynamic_slice_in_dim(span_normed, lax.axis_index("tp") * rows_here, rows_here)
    hidden = jax.nn.gelu(
        jnp.dot(span_normed, w_up, preferred_element_type=jnp.float32) + b_up,
        approximate=False,
    ).astype(jnp.bfloat16)
    partial = jnp.dot(hidden, w_down, preferred_element_type=jnp.float32).astype(jnp.bfloat16)
    partial = lax.all_to_all(
        partial.reshape((n_tp, -1) + partial.shape[1:]), "tp", split_axis=0, concat_axis=0, tiled=True
    )
    summed = jnp.sum(partial.astype(jnp.float32), axis=0) + b_down + normed.astype(jnp.float32)
    return layer_norm(summed, ln2_gain, ln2_bias).astype(jnp.bfloat16)


def solution(mesh):
    placed = (
        P(("req", "tp"), None),
        P(None, None, "tp"),
        P("tp", None),
        P(None, "tp"),
        P("tp"),
        P("tp", None),
        P(),
        P(),
        P(),
        P(),
        P(),
        P(None, None, "req", "tp"),
        P(),
        P(),
    )
    return jax.shard_map(
        shards, mesh=mesh, in_specs=placed, out_specs=P(("req", "tp"), None), check_vma=False
    )
```

```python
import jax
import jax.numpy as jnp
from jax import lax
from jax.experimental import pallas as pl
from jax.experimental.pallas import tpu as pltpu
from jax.sharding import PartitionSpec as P

HEAD_DIM = 64
BLEND_STEP = 8

masked_score = -1e30


def layer_norm(values, gain, bias):
    centre = jnp.mean(values, axis=-1, keepdims=True)
    centred = values - centre
    variance = jnp.mean(centred * centred, axis=-1, keepdims=True)
    return centred * lax.rsqrt(variance + 1e-05) * gain + bias


def partial_attention(queries, key_rows, value_rows, allowed):
    scores = jnp.einsum(
        "chd,nhd->hcn", queries, key_rows, preferred_element_type=jnp.float32
    ) * queries.shape[-1] ** (-0.5)
    scores = jnp.where(allowed[None], scores, masked_score)
    peaks = jnp.max(scores, axis=-1)
    weights = jnp.where(allowed[None], jnp.exp(scores - peaks[..., None]), 0.0).astype(jnp.bfloat16)
    weight_sums = jnp.sum(weights.astype(jnp.float32), axis=-1)
    blended = jnp.einsum("hcn,nhd->chd", weights, value_rows, preferred_element_type=jnp.float32)
    return (peaks.T, weight_sums.T, blended.reshape(blended.shape[0], -1))


def merge_axis(peaks, weight_sums, blended, axis):
    highest = jnp.max(peaks, axis=axis, keepdims=True)
    factors = jnp.exp(peaks - highest)
    sums_out = jnp.sum(factors * weight_sums, axis=axis)
    spread = jnp.repeat(factors, blended.shape[-1] // peaks.shape[-1], axis=-1)
    blend_out = jnp.sum(spread * blended, axis=axis)
    return (jnp.squeeze(highest, axis=axis), sums_out, blend_out)


def score_kernel(count_ref, qt_ref, k_ref, w_ref, peak_ref):
    block = pl.program_id(0)
    heads = qt_ref.shape[0]
    width = k_ref.shape[1]
    start = block * width
    scale = HEAD_DIM ** (-0.5)

    def step(masked):
        allowed = start + lax.broadcasted_iota(jnp.int32, (width, 1), 0) < count_ref[0]
        for head in range(heads):
            raw = jnp.dot(k_ref[0], qt_ref[head], preferred_element_type=jnp.float32)
            if masked:
                raw = jnp.where(allowed, raw, masked_score)
            top = jnp.max(raw, axis=0, keepdims=True)
            weights = jnp.exp((raw - top) * scale)
            if masked:
                weights = jnp.where(allowed, weights, 0.0)
            w_ref[0, head] = weights.astype(jnp.bfloat16)
            peak_ref[0, head] = top * scale

    full = start + width <= count_ref[0]
    some = start < count_ref[0]

    @pl.when(full)
    def _():
        step(False)

    @pl.when(some & jnp.logical_not(full))
    def _():
        step(True)

    @pl.when(jnp.logical_not(some))
    def _():
        w_ref[...] = jnp.zeros_like(w_ref)
        peak_ref[...] = jnp.full_like(peak_ref, masked_score)


def blend_kernel(count_ref, w_ref, block_peak_ref, vt_ref, acc_ref, peak_ref):
    step = pl.program_id(0)
    per_step, heads = w_ref.shape[0], w_ref.shape[1]
    width = vt_ref.shape[2]

    @pl.when(step == 0)
    def _():
        acc_ref[...] = jnp.zeros_like(acc_ref)
        peak_ref[...] = jnp.full_like(peak_ref, masked_score)

    for sub in range(per_step):
        start = (step * per_step + sub) * width

        @pl.when(start < count_ref[0])
        def _():
            row = lax.broadcasted_iota(jnp.int32, (vt_ref.shape[1], 1), 0)
            for head in range(heads):
                own = (row >= head * HEAD_DIM) & (row < (head + 1) * HEAD_DIM)
                values = jnp.where(own, vt_ref[sub], jnp.ones_like(vt_ref[sub]))
                blend = jnp.dot(values, w_ref[sub, head], preferred_element_type=jnp.float32)
                peak = block_peak_ref[sub, head]
                old = peak_ref[head]
                new = jnp.maximum(old, peak)
                peak_ref[head] = new
                acc_ref[head] = acc_ref[head] * jnp.exp(old - new) + blend * jnp.exp(peak - new)


def block_weights(queries, own_keys, cached_count):
    span, width = queries.shape
    total_blocks, block_width = own_keys.shape[0], own_keys.shape[1]
    heads = width // HEAD_DIM
    row = jnp.arange(width)[None, :, None] // HEAD_DIM
    padded = jnp.where(row == jnp.arange(heads)[:, None, None], queries.T[None], jnp.zeros_like(queries.T)[None])
    grid_spec = pltpu.PrefetchScalarGridSpec(
        num_scalar_prefetch=1,
        grid=(total_blocks,),
        in_specs=[
            pl.BlockSpec((heads, width, span), lambda b, c: (0, 0, 0)),
            pl.BlockSpec((1, block_width, width), lambda b, c: (b, 0, 0)),
        ],
        out_specs=[
            pl.BlockSpec((1, heads, block_width, span), lambda b, c: (b, 0, 0, 0)),
            pl.BlockSpec((1, heads, 1, span), lambda b, c: (b, 0, 0, 0)),
        ],
    )
    return pl.pallas_call(
        score_kernel,
        grid_spec=grid_spec,
        out_shape=[
            jax.ShapeDtypeStruct((total_blocks, heads, block_width, span), jnp.bfloat16),
            jax.ShapeDtypeStruct((total_blocks, heads, 1, span), jnp.float32),
        ],
        compiler_params=pltpu.CompilerParams(dimension_semantics=("arbitrary",)),
        cost_estimate=pl.CostEstimate(
            flops=2 * span * block_width * width * heads * total_blocks,
            transcendentals=heads * span * block_width * total_blocks,
            bytes_accessed=own_keys.size * 2 + total_blocks * heads * span * block_width * 2,
        ),
    )(jnp.reshape(cached_count, (1,)), padded, own_keys)


def cache_partials(weights, block_peaks, own_value_rows, cached_count):
    total_blocks, heads, block_width, span = weights.shape
    width = own_value_rows.shape[1]
    per_step = BLEND_STEP if total_blocks % BLEND_STEP == 0 else 1
    grid_spec = pltpu.PrefetchScalarGridSpec(
        num_scalar_prefetch=1,
        grid=(total_blocks // per_step,),
        in_specs=[
            pl.BlockSpec((per_step, heads, block_width, span), lambda b, c: (b, 0, 0, 0)),
            pl.BlockSpec((per_step, heads, 1, span), lambda b, c: (b, 0, 0, 0)),
            pl.BlockSpec((per_step, width, block_width), lambda b, c: (b, 0, 0)),
        ],
        out_specs=[
            pl.BlockSpec((heads, width, span), lambda b, c: (0, 0, 0)),
            pl.BlockSpec((heads, 1, span), lambda b, c: (0, 0, 0)),
        ],
    )
    acc, peaks = pl.pallas_call(
        blend_kernel,
        grid_spec=grid_spec,
        out_shape=[
            jax.ShapeDtypeStruct((heads, width, span), jnp.float32),
            jax.ShapeDtypeStruct((heads, 1, span), jnp.float32),
        ],
        compiler_params=pltpu.CompilerParams(dimension_semantics=("arbitrary",)),
        cost_estimate=pl.CostEstimate(
            flops=2 * span * block_width * width * heads * total_blocks,
            transcendentals=2 * heads * span * total_blocks,
            bytes_accessed=weights.size * 2 + own_value_rows.size * 2 + heads * span * width * 4,
        ),
    )(jnp.reshape(cached_count, (1,)), weights, block_peaks, own_value_rows)
    spare = [((head + 1) % heads) * HEAD_DIM for head in range(heads)]
    blended = jnp.concatenate([acc[head, head * HEAD_DIM : (head + 1) * HEAD_DIM, :] for head in range(heads)], axis=0).T
    sums = jnp.stack([acc[head, spare[head], :] for head in range(heads)], axis=1)
    return peaks[:, 0, :].T, sums, blended


def shards(
    tokens,
    w_qkv,
    w_out,
    w_up,
    b_up,
    w_down,
    b_down,
    ln1_gain,
    ln1_bias,
    ln2_gain,
    ln2_bias,
    kv_cache,
    cache_len,
    span_len,
):
    width_here = w_qkv.shape[2]
    heads_here = width_here // HEAD_DIM
    where_req = lax.axis_index("req")

    own_keys = lax.all_to_all(kv_cache[0], "req", split_axis=0, concat_axis=0, tiled=True)
    own_keys, value_rows = lax.optimization_barrier((own_keys, jnp.swapaxes(kv_cache[1], 1, 2)))
    own_value_rows = lax.all_to_all(value_rows, "req", split_axis=0, concat_axis=0, tiled=True)

    span_rows = lax.all_gather(tokens, "tp", axis=0, tiled=True)
    flat_qkv = w_qkv.reshape(w_qkv.shape[0], 3 * width_here)
    heads_qkv = jnp.dot(span_rows, flat_qkv, preferred_element_type=jnp.float32).astype(jnp.bfloat16)
    span = heads_qkv.shape[0]
    local_shape = (span, heads_here, HEAD_DIM)
    queries = heads_qkv[:, :width_here].reshape(local_shape)
    fresh_keys = heads_qkv[:, width_here : 2 * width_here].reshape(local_shape)
    fresh_values = heads_qkv[:, 2 * width_here :].reshape(local_shape)

    full_out = lax.all_gather(w_out, "tp", axis=0, tiled=True)

    fresh_count = span_len[where_req]
    cached_count = cache_len[where_req]
    positions = jnp.arange(span, dtype=jnp.int32)
    allowed = (positions[None, :] <= positions[:, None]) & (positions[None, :] < fresh_count)
    fresh = partial_attention(queries, fresh_keys, fresh_values, allowed)

    weights, block_peaks = block_weights(heads_qkv[:, :width_here], own_keys, cached_count)
    peaks, weight_sums, blended = cache_partials(weights, block_peaks, own_value_rows, cached_count)
    peaks, weight_sums, blended = merge_axis(
        jnp.stack([fresh[0], peaks]),
        jnp.stack([fresh[1], weight_sums]),
        jnp.stack([fresh[2], blended]),
        0,
    )
    attention = (blended / jnp.repeat(weight_sums, HEAD_DIM, axis=-1)).astype(jnp.bfloat16)
    n_tp = lax.axis_size("tp")
    attention = lax.all_to_all(
        jnp.broadcast_to(attention[None], (n_tp,) + attention.shape), "tp", split_axis=0, concat_axis=2, tiled=True
    ).reshape(span, -1)

    projected = jnp.dot(attention, full_out, preferred_element_type=jnp.float32)
    span_normed = layer_norm(span_rows.astype(jnp.float32) + projected, ln1_gain, ln1_bias).astype(jnp.bfloat16)
    rows_here = tokens.shape[0]
    normed = lax.dynamic_slice_in_dim(span_normed, lax.axis_index("tp") * rows_here, rows_here)
    hidden = jax.nn.gelu(
        jnp.dot(span_normed, w_up, preferred_element_type=jnp.float32) + b_up,
        approximate=False,
    ).astype(jnp.bfloat16)
    partial = jnp.dot(hidden, w_down, preferred_element_type=jnp.float32).astype(jnp.bfloat16)
    partial = lax.all_to_all(
        partial.reshape((n_tp, -1) + partial.shape[1:]), "tp", split_axis=0, concat_axis=0, tiled=True
    )
    summed = jnp.sum(partial.astype(jnp.float32), axis=0) + b_down + normed.astype(jnp.float32)
    return layer_norm(summed, ln2_gain, ln2_bias).astype(jnp.bfloat16)


def solution(mesh):
    placed = (
        P(("req", "tp"), None),
        P(None, None, "tp"),
        P("tp", None),
        P(None, "tp"),
        P("tp"),
        P("tp", None),
        P(),
        P(),
        P(),
        P(),
        P(),
        P(None, None, "req", "tp"),
        P(),
        P(),
    )
    return jax.shard_map(
        shards, mesh=mesh, in_specs=placed, out_specs=P(("req", "tp"), None), check_vma=False
    )
```
